32 devices in a mesh: dp: 8 (over z, x), mp: 4 (over y, core).
Axes of the slice: x: 2, y: 2, z: 4, core: 2. Of those that a mesh axis runs over, the one named last changes fastest.
Arguments:
- queries: bfloat16 [1024, 4, 8192], P('dp', None, 'mp'), may hold values from -6 to 6
- fresh_key_value: bfloat16 [1024, 4, 2, 8, 128], P('dp', None, None, 'mp'), may hold values from -6 to 6
- key_value_pool: bfloat16 [4096, 2, 8, 16, 128], P('dp', None, 'mp'), may hold values from -6 to 6
- block_position_map: int32 [4096], replicated, may hold values from 0 to 4095
- request_blocks: int32 [1024, 4], P('dp'), may hold values from 0 to 4095, as said below
- live_prefix_length: int32 [1024], P('dp'), may hold values from 1 to 64, as said below
- request_adapter: int32 [1024, 1], P('dp'), may hold values from 0 to 15; in each aligned block of 128 rows (0 to 127, 128 to 255, ...) at most 8 rows name the same one
- output_weight: bfloat16 [8192, 8192], P('mp'), may hold values from -0.0625 to 0.0625
- adapter_down_panels: bfloat16 [16, 64, 8192], P('dp', None, 'mp'), may hold values from -0.0625 to 0.0625
- adapter_up_panels: bfloat16 [16, 64, 8192], P('dp', None, 'mp'), may hold values from -0.75 to 0.75
Outputs:
- layer_out: bfloat16 [1024, 4, 8192], P('dp', None, 'mp')
The draws below stay inside these ranges and needn't reach their ends.
Inputs may be any that keep to these rules, and one draw needn't show every extreme that they name: `request_blocks`: every logical block is given a distinct pool position. The 512 entries of one index of dp name 256 distinct blocks, each exactly twice. Through the owner map at most 64 distinct blocks of one index of dp, and so at most 128 of its entries, lie on one pool owner (pool positions owner * 512 to owner * 512 + 511); one pool owner holds exactly 64 distinct blocks of every index of dp. `live_prefix_length`: all requests of some index of dp have the full 4 * 16 prefix tokens. `request_adapter`: among the 128 requests of one index of dp no adapter appears more than 8 times, and that many is reached.
All inputs are finite; a program needn't handle non-finite values.
Results may differ from the reference program's by a relative error of at most 0.008.
Values may be sent and summed in bfloat16 or wider, within the bound.
No kernel may reach another device: no remote copies, remote signals or barrier semaphores. Data moves between devices by JAX's collectives and lax.ppermute only.
A program may use at most 192 MiB of HBM per device.

```python
import math
import jax
import jax.numpy as jnp
import numpy as np
from jax import lax

MODEL_WIDTH = 8192
QUERY_HEADS = 64
KVH = 8
HEAD_SIZE = 128
ADAPTER_RANK = 64
BLK = 16
STEPS = 4
MAXB = 4
REQ_DEV = 128
POOL_DEV = 512
ACAP = 8
REQUESTS = 1024
POOL = 4096
ADAPTER_COUNT = 16
DCAP = 64
N_DP = 8


def pool_layout(key):
    owners = POOL // POOL_DEV
    block_position_map = jax.random.permutation(jax.random.fold_in(key, 11), POOL).astype(jnp.int32)
    busy_owner = jax.random.randint(jax.random.fold_in(key, 12), (), 0, owners)

    def device_entries(device):
        dev_key = jax.random.fold_in(jax.random.fold_in(key, 13), device)
        subkeys = jax.random.split(dev_key, owners + 2)
        local_rows = jax.vmap(lambda subkey: jax.random.permutation(subkey, POOL_DEV)[:DCAP])(subkeys[:owners])
        slot_owner = jnp.arange(owners)[:, None] * jnp.ones((1, DCAP), jnp.int32)
        spots = (slot_owner * POOL_DEV + local_rows).reshape(-1)
        shuffled = jax.random.permutation(subkeys[owners], owners * DCAP).astype(jnp.int32)
        ranking = jnp.where(slot_owner.reshape(-1) == busy_owner, shuffled - owners * DCAP, shuffled)
        chosen = spots[jnp.argsort(ranking)[:REQ_DEV * MAXB // 2]]
        doubled = jnp.concatenate([chosen, chosen])
        return doubled[jax.random.permutation(subkeys[owners + 1], REQ_DEV * MAXB)]
    positions = jax.vmap(device_entries)(jnp.arange(owners))
    inverse = jnp.argsort(block_position_map).astype(jnp.int32)
    blocks = inverse[positions].reshape(REQUESTS, MAXB)
    return (block_position_map, blocks.astype(jnp.int32))


def draw_block_position_map(key, part):
    return pool_layout(key)[0]


def draw_request_blocks(key, part):
    return pool_layout(key)[1]


def draw_live_prefix_length(key, part):
    owners = REQUESTS // REQ_DEV
    lengths = jax.random.randint(jax.random.fold_in(key, 21), (REQUESTS,), 1, MAXB * BLK + 1)
    full_device = jax.random.randint(jax.random.fold_in(key, 22), (), 0, owners)
    device = jnp.arange(REQUESTS) // REQ_DEV
    return jnp.where(device == full_device, MAXB * BLK, lengths).astype(jnp.int32)


def draw_queries(key, part):
    shape = (REQUESTS, STEPS, QUERY_HEADS, HEAD_SIZE)
    values = jnp.clip(jax.random.normal(jax.random.fold_in(key, 34), shape, jnp.float32), -6.0, 6.0)
    return values.reshape(REQUESTS, STEPS, QUERY_HEADS * HEAD_SIZE).astype(jnp.bfloat16)


def draw_key_value_pool(key, part):
    shape = (POOL, 2, KVH, BLK, HEAD_SIZE)
    values = jnp.clip(jax.random.normal(jax.random.fold_in(key, 44), shape, jnp.float32), -6.0, 6.0)
    return values.astype(jnp.bfloat16)


def steps_of(rng, extent, shards, low, top_value):
    factor_of = 1.0
    for axis_at, parts in shards:
        steps = jax.random.uniform(jax.random.fold_in(jax.random.fold_in(rng, 6), axis_at), (parts,), jnp.float32, low / len(shards), top_value / len(shards))
        factor_of = factor_of * jnp.repeat(jnp.exp(steps), extent[axis_at] // parts).reshape((-1,) + (1,) * (len(extent) - 1 - axis_at))
    return factor_of


def deal_out(rng, own, number, rows, number_of, top, limit, skew):
    order = jax.random.permutation(rng, number_of)
    heavy_load, ordinary = shares(number_of, rows * top, limit, skew, True), shares(number_of, rows * top, limit, skew, False)
    places = jnp.arange(number_of)

    def named(sizes, rotation):
        used = int((sizes > 0).sum())
        fixed = max(1, used // 4)
        shifted = fixed + (places - fixed + rotation * (used - fixed)) % max(1, number_of - fixed)
        return jnp.zeros((number_of,), jnp.int32).at[order[jnp.where(places < fixed, places, shifted)]].set(jnp.asarray(sizes, jnp.int32))

    sizes = jnp.where(number % 4 == 0, named(heavy_load, number // 4), named(ordinary, number - number // 4 - 1))
    mixed = jax.random.permutation(jax.random.fold_in(own, 3), number_of)
    giver, receiver = mixed[0:number_of // 2 * 2:2], mixed[1:number_of // 2 * 2:2]
    room = jnp.minimum(sizes[giver] - 1, limit - sizes[receiver]) // 2
    room = jnp.where((giver == order[0]) | (receiver == order[0]) | (sizes[receiver] == 0), 0, jnp.maximum(room, 0))
    shifted = jax.random.randint(jax.random.fold_in(own, 4), (number_of // 2,), 0, 1 << 20) % (room + 1)
    sizes = sizes.at[giver].add(-shifted).at[receiver].add(shifted)
    members = jnp.searchsorted(jnp.cumsum(sizes), jnp.arange(rows * top), side="right").astype(jnp.int32)
    grid = members.reshape(top, rows).T
    grid = grid[jax.random.permutation(jax.random.fold_in(own, 1), rows)]
    rotation = jax.random.randint(jax.random.fold_in(own, 2), (rows, 1), 0, top)
    return jnp.take_along_axis(grid, (jnp.arange(top)[None, :] + rotation) % top, axis=1)


def shares(amount, total, bound, lean, full):
    weights = [(1 << 20) // math.isqrt(grade ** lean) + 1 for grade in range(1, amount + 1)]
    largest = bound if full else min(bound, max(-(-total // amount), total * weights[0] // sum(weights)))
    least = 1 if total - largest >= amount - 1 else 0
    counts, surplus = [largest] + [least] * (amount - 1), total - largest - least * (amount - 1)
    while surplus > 0:
        free = [i for i in range(1, amount) if counts[i] < largest] or [i for i in range(1, amount) if counts[i] < bound]
        whole, left = sum([weights[i] for i in free]), surplus
        for i in free:
            addition = min(bound - counts[i], max(1, left * weights[i] // whole), surplus)
            counts[i] = counts[i] + addition
            surplus = surplus - addition
    return np.array(counts)


def scatter_about(rng, shape, scale, limit, cuts=(), dtype=jnp.bfloat16):
    drawn = scale * jax.random.normal(rng, shape, jnp.float32)
    if cuts:
        drawn = drawn * steps_of(rng, shape, cuts, -0.22, 0.18)
    return jnp.clip(drawn, -limit, limit).astype(dtype)


def setup_inputs(seed: int = 0) -> dict:
    splits = jax.random.split(jax.random.key(seed), 11)
    queries = draw_queries(jax.random.fold_in(splits[10], 71), 0)
    fresh_key_value = scatter_about(splits[1], (REQUESTS, STEPS, 2, KVH, HEAD_SIZE), 1.0, 6.0, ((0, 8), (3, 4)))
    key_value_pool = draw_key_value_pool(jax.random.fold_in(splits[10], 71), 0)
    block_position_map = draw_block_position_map(jax.random.fold_in(splits[10], 71), 0)
    request_blocks = draw_request_blocks(jax.random.fold_in(splits[10], 71), 0)
    live_prefix_length = draw_live_prefix_length(jax.random.fold_in(splits[10], 71), 0)
    request_adapter_keys = jax.random.split(jax.random.fold_in(splits[6], 1), REQUESTS // REQ_DEV)
    request_adapter_turns = jax.random.permutation(jax.random.fold_in(splits[6], 3), REQUESTS // REQ_DEV)
    request_adapter = jax.vmap(lambda own, number: deal_out(jax.random.fold_in(splits[6], 2), own, number, REQ_DEV, ADAPTER_COUNT, 1, ACAP, 2))(request_adapter_keys, request_adapter_turns).reshape((REQUESTS, 1))
    output_weight = scatter_about(splits[7], (QUERY_HEADS * HEAD_SIZE, MODEL_WIDTH), (QUERY_HEADS * HEAD_SIZE) ** -0.5, 0.0625, ((0, 4),))
    adapter_down_panels = scatter_about(splits[8], (ADAPTER_COUNT, ADAPTER_RANK, QUERY_HEADS * HEAD_SIZE), (QUERY_HEADS * HEAD_SIZE) ** -0.5, 0.0625, ((0, 8), (2, 4)))
    adapter_up_panels = scatter_about(splits[9], (ADAPTER_COUNT, ADAPTER_RANK, MODEL_WIDTH), ADAPTER_RANK ** -0.5, 0.75, ((0, 8), (2, 4)))
    return {"queries": queries, "fresh_key_value": fresh_key_value, "key_value_pool": key_value_pool, "block_position_map": block_position_map, "request_blocks": request_blocks, "live_prefix_length": live_prefix_length, "request_adapter": request_adapter, "output_weight": output_weight, "adapter_down_panels": adapter_down_panels, "adapter_up_panels": adapter_up_panels}


ADAPTER_SCALE = 2.0


def reference(queries, fresh_key_value, key_value_pool, block_position_map, request_blocks, live_prefix_length, request_adapter, output_weight, adapter_down_panels, adapter_up_panels):
    group_size = QUERY_HEADS // KVH
    score_scale = HEAD_SIZE ** -0.5
    token_index = jnp.arange(MAXB)[:, None] * BLK + jnp.arange(BLK)[None, :]
    causal = jnp.arange(STEPS)[None, :] <= jnp.arange(STEPS)[:, None]

    def one_block(packed):
        query_rows, new_rows, block_rows, lengths, adapter_table = packed
        row_count = query_rows.shape[0]
        query = query_rows.astype(jnp.float32).reshape(row_count, STEPS, KVH, group_size, HEAD_SIZE)
        prefix = key_value_pool[block_position_map[block_rows]].astype(jnp.float32)
        prefix_scores = jnp.einsum('qsghd,qbgtd->qsghbt', query, prefix[:, :, 0]) * score_scale
        live_mask = token_index[None] < lengths[:, None, None]
        prefix_scores = jnp.where(live_mask[:, None, None, None], prefix_scores, -jnp.inf)
        fresh = new_rows.astype(jnp.float32)
        fresh_scores = jnp.einsum('qsghd,qjgd->qsghj', query, fresh[:, :, 0]) * score_scale
        fresh_scores = jnp.where(causal[None, :, None, None, :], fresh_scores, -jnp.inf)
        row_top = jnp.maximum(jnp.max(prefix_scores, axis=(4, 5)), jnp.max(fresh_scores, axis=4))
        prefix_w = jnp.exp(prefix_scores - row_top[..., None, None])
        fresh_w = jnp.exp(fresh_scores - row_top[..., None])
        row_total = jnp.sum(prefix_w, axis=(4, 5)) + jnp.sum(fresh_w, axis=4)
        prefix_p = (prefix_w / row_total[..., None, None]).astype(jnp.bfloat16)
        fresh_p = (fresh_w / row_total[..., None]).astype(jnp.bfloat16)
        attended = jnp.einsum('qsghbt,qbgtd->qsghd', prefix_p.astype(jnp.float32), prefix[:, :, 1])
        attended = attended + jnp.einsum('qsghj,qjgd->qsghd', fresh_p.astype(jnp.float32), fresh[:, :, 1])
        attended = attended.astype(jnp.bfloat16).reshape(row_count, STEPS, QUERY_HEADS * HEAD_SIZE)
        base_product = jnp.dot(attended.reshape(row_count * STEPS, QUERY_HEADS * HEAD_SIZE), output_weight, preferred_element_type=jnp.float32)
        base_product = base_product.reshape(row_count, STEPS, MODEL_WIDTH)
        picked_down = adapter_down_panels[adapter_table].astype(jnp.float32)
        rank_features = jnp.einsum('qsf,qrf->qsr', attended.astype(jnp.float32), picked_down).astype(jnp.bfloat16)
        picked_up = adapter_up_panels[adapter_table].astype(jnp.float32)
        adapter_product = (jnp.einsum('mgh,mhl->mgl', rank_features.astype(jnp.float32), picked_up) * ADAPTER_SCALE).astype(jnp.bfloat16)
        return (base_product + adapter_product.astype(jnp.float32)).astype(jnp.bfloat16)

    packed = (
        queries.reshape(N_DP, REQ_DEV, STEPS, QUERY_HEADS * HEAD_SIZE),
        fresh_key_value.reshape(N_DP, REQ_DEV, STEPS, 2, KVH, HEAD_SIZE),
        request_blocks.reshape(N_DP, REQ_DEV, MAXB),
        live_prefix_length.reshape(N_DP, REQ_DEV),
        request_adapter[:, 0].reshape(N_DP, REQ_DEV),
    )
    return lax.map(one_block, packed).reshape(REQUESTS, STEPS, MODEL_WIDTH)
```

```python
import jax
import jax.numpy as jnp
from jax import lax
from jax.sharding import PartitionSpec as P

ADAPTER_SCALE = 2.0


def shards(
    queries,
    fresh_key_value,
    key_value_pool,
    block_position_map,
    request_blocks,
    live_prefix_length,
    request_adapter,
    output_weight,
    adapter_down_panels,
    adapter_up_panels,
):
    owners = lax.axis_size("dp")
    req_dev, step_count, query_width = queries.shape
    kv_heads = fresh_key_value.shape[3]
    head_dim = fresh_key_value.shape[4]
    pool_dev = key_value_pool.shape[0]
    block_len = key_value_pool.shape[3]
    blocks_per = request_blocks.shape[1]
    entries = req_dev * blocks_per
    out_width = output_weight.shape[1]
    owner_range = jnp.arange(owners)
    positions = jnp.take(block_position_map, request_blocks.reshape(entries))
    target = positions // pool_dev
    local_slot = positions % pool_dev
    capacity = entries // owners
    entry_ids = jnp.arange(entries)
    same_block = positions[:, None] == positions[None, :]
    earlier = entry_ids[None, :] < entry_ids[:, None]
    first = jnp.logical_not(jnp.any(same_block & earlier, axis=1))
    same_owner = target[:, None] == target[None, :]
    rank = jnp.sum((same_owner & earlier & first[None, :]).astype(jnp.int32), axis=1)
    first_of = same_block & first[None, :]
    slot_index = jnp.sum(jnp.where(first_of, rank[None, :], 0), axis=1)
    key = jnp.where(first, target * capacity + rank, -1)
    table_ids = jnp.arange(owners * capacity)
    wish_table = jnp.sum(
        jnp.where(key[:, None] == table_ids[None, :], local_slot[:, None], 0), axis=0
    ).reshape(owners, capacity)
    wanted = lax.all_to_all(wish_table, "dp", split_axis=0, concat_axis=0, tiled=True)
    served = jnp.take(key_value_pool, wanted.reshape(-1), axis=0).reshape(
        (owners, capacity) + key_value_pool.shape[1:]
    )
    fetched = lax.all_to_all(served, "dp", split_axis=0, concat_axis=0, tiled=True)
    flat_rows = fetched.reshape((owners * capacity,) + key_value_pool.shape[1:])
    own_blocks = jnp.take(flat_rows, target * capacity + slot_index, axis=0)
    own_blocks = own_blocks.reshape((req_dev, blocks_per) + key_value_pool.shape[1:])
    group_size = query_width // (kv_heads * head_dim)
    query = queries.reshape(req_dev, step_count, kv_heads, group_size, head_dim)
    score_scale = head_dim ** (-0.5)
    prefix_scores = (
        jnp.einsum(
            "qsghd,qbgtd->qsghbt", query, own_blocks[:, :, 0], preferred_element_type=jnp.float32
        )
        * score_scale
    )
    token_index = jnp.arange(blocks_per)[:, None] * block_len + jnp.arange(block_len)[None, :]
    live_mask = token_index[None] < live_prefix_length[:, None, None]
    prefix_scores = jnp.where(live_mask[:, None, None, None], prefix_scores, -jnp.inf)
    fresh_scores = (
        jnp.einsum(
            "qsghd,qjgd->qsghj", query, fresh_key_value[:, :, 0], preferred_element_type=jnp.float32
        )
        * score_scale
    )
    causal = jnp.arange(step_count)[None, :] <= jnp.arange(step_count)[:, None]
    fresh_scores = jnp.where(causal[None, :, None, None, :], fresh_scores, -jnp.inf)
    row_top = jnp.maximum(jnp.max(prefix_scores, axis=(4, 5)), jnp.max(fresh_scores, axis=4))
    prefix_w = jnp.exp(prefix_scores - row_top[..., None, None])
    fresh_w = jnp.exp(fresh_scores - row_top[..., None])
    row_total = jnp.sum(prefix_w, axis=(4, 5)) + jnp.sum(fresh_w, axis=4)
    prefix_p = (prefix_w / row_total[..., None, None]).astype(jnp.bfloat16)
    fresh_p = (fresh_w / row_total[..., None]).astype(jnp.bfloat16)
    attended = jnp.einsum(
        "qsghbt,qbgtd->qsghd", prefix_p, own_blocks[:, :, 1], preferred_element_type=jnp.float32
    )
    attended = attended + jnp.einsum(
        "qsghj,qjgd->qsghd", fresh_p, fresh_key_value[:, :, 1], preferred_element_type=jnp.float32
    )
    attended = attended.astype(jnp.bfloat16).reshape(req_dev, step_count, query_width)
    base_product = jnp.dot(
        attended.reshape(req_dev * step_count, query_width),
        output_weight,
        preferred_element_type=jnp.float32,
    )
    base_product = base_product.reshape(req_dev, step_count, out_width)
    adapter = request_adapter[:, 0]
    single_panel = lax.all_gather(adapter_down_panels, "dp", axis=0, tiled=True)
    panel_count = single_panel.shape[0]
    hit_mask = (adapter[:, None] == jnp.arange(panel_count)[None, :]).astype(jnp.float32)
    every_rank = jnp.einsum(
        "qsf,nrf->qsnr", attended, single_panel, preferred_element_type=jnp.float32
    )
    rank_part = jnp.einsum("qsnr,qn->qsr", every_rank, hit_mask)
    rank_sum = lax.psum(rank_part, "mp").astype(jnp.bfloat16)
    single_panel = lax.all_gather(adapter_up_panels, "dp", axis=0, tiled=True)
    panel_count = single_panel.shape[0]
    hit_mask = (adapter[:, None] == jnp.arange(panel_count)[None, :]).astype(jnp.bfloat16)
    selected_panel = rank_sum[:, :, None, :] * hit_mask[:, None, :, None]
    adapter_sum = jnp.einsum(
        "utja,jam->utm", selected_panel, single_panel, preferred_element_type=jnp.float32
    )
    adapter_output = (adapter_sum * ADAPTER_SCALE).astype(jnp.bfloat16)
    summed_output = lax.psum_scatter(base_product, "mp", scatter_dimension=2, tiled=True)
    return (summed_output + adapter_output.astype(jnp.float32)).astype(jnp.bfloat16)


def solution(mesh):
    in_specs = (
        P("dp", None, "mp"),
        P("dp", None, None, "mp", None),
        P("dp", None, "mp", None, None),
        P(),
        P("dp", None),
        P("dp"),
        P("dp", None),
        P("mp", None),
        P("dp", None, "mp"),
        P("dp", None, "mp"),
    )
    out_specs = P("dp", None, "mp")
    return jax.shard_map(shards, mesh=mesh, in_specs=in_specs, out_specs=out_specs, check_vma=False)
```

```python
import jax
import jax.numpy as jnp
from jax import lax
from jax.sharding import PartitionSpec as P

ADAPTER_SCALE = 2.0


def shards(
    queries,
    fresh_key_value,
    key_value_pool,
    block_position_map,
    request_blocks,
    live_prefix_length,
    request_adapter,
    output_weight,
    adapter_down_panels,
    adapter_up_panels,
):
    owners = lax.axis_size("dp")
    req_dev, step_count, query_width = queries.shape
    kv_heads = fresh_key_value.shape[3]
    head_dim = fresh_key_value.shape[4]
    pool_dev = key_value_pool.shape[0]
    block_len = key_value_pool.shape[3]
    blocks_per = request_blocks.shape[1]
    entries = req_dev * blocks_per
    out_width = output_weight.shape[1]
    owner_range = jnp.arange(owners)
    positions = jnp.take(block_position_map, request_blocks.reshape(entries))
    target = positions // pool_dev
    local_slot = positions % pool_dev
    capacity = entries // owners
    entry_ids = jnp.arange(entries)
    same_block = positions[:, None] == positions[None, :]
    earlier = entry_ids[None, :] < entry_ids[:, None]
    first = jnp.logical_not(jnp.any(same_block & earlier, axis=1))
    same_owner = target[:, None] == target[None, :]
    rank = jnp.sum((same_owner & earlier & first[None, :]).astype(jnp.int32), axis=1)
    first_of = same_block & first[None, :]
    slot_index = jnp.sum(jnp.where(first_of, rank[None, :], 0), axis=1)
    key = jnp.where(first, target * capacity + rank, -1)
    table_ids = jnp.arange(owners * capacity)
    wish_table = jnp.sum(
        jnp.where(key[:, None] == table_ids[None, :], local_slot[:, None], 0), axis=0
    ).reshape(owners, capacity)
    wanted = lax.all_to_all(wish_table, "dp", split_axis=0, concat_axis=0, tiled=True)
    served = jnp.take(key_value_pool, wanted.reshape(-1), axis=0).reshape(
        (owners, capacity) + key_value_pool.shape[1:]
    )
    fetched = lax.all_to_all(served, "dp", split_axis=0, concat_axis=0, tiled=True)
    fetched, adapter_down_panels, adapter_up_panels = lax.optimization_barrier(
        (fetched, adapter_down_panels, adapter_up_panels)
    )
    flat_rows = fetched.reshape((owners * capacity,) + key_value_pool.shape[1:])
    own_blocks = jnp.take(flat_rows, target * capacity + slot_index, axis=0)
    own_blocks = own_blocks.reshape((req_dev, blocks_per) + key_value_pool.shape[1:])
    group_size = query_width // (kv_heads * head_dim)
    query = queries.reshape(req_dev, step_count, kv_heads, group_size, head_dim)
    score_scale = head_dim ** (-0.5)
    prefix_scores = (
        jnp.einsum(
            "qsghd,qbgtd->qsghbt", query, own_blocks[:, :, 0], preferred_element_type=jnp.float32
        )
        * score_scale
    )
    token_index = jnp.arange(blocks_per)[:, None] * block_len + jnp.arange(block_len)[None, :]
    live_mask = token_index[None] < live_prefix_length[:, None, None]
    prefix_scores = jnp.where(live_mask[:, None, None, None], prefix_scores, -jnp.inf)
    fresh_scores = (
        jnp.einsum(
            "qsghd,qjgd->qsghj", query, fresh_key_value[:, :, 0], preferred_element_type=jnp.float32
        )
        * score_scale
    )
    causal = jnp.arange(step_count)[None, :] <= jnp.arange(step_count)[:, None]
    fresh_scores = jnp.where(causal[None, :, None, None, :], fresh_scores, -jnp.inf)
    row_top = jnp.maximum(jnp.max(prefix_scores, axis=(4, 5)), jnp.max(fresh_scores, axis=4))
    prefix_w = jnp.exp(prefix_scores - row_top[..., None, None])
    fresh_w = jnp.exp(fresh_scores - row_top[..., None])
    row_total = jnp.sum(prefix_w, axis=(4, 5)) + jnp.sum(fresh_w, axis=4)
    prefix_p = (prefix_w / row_total[..., None, None]).astype(jnp.bfloat16)
    fresh_p = (fresh_w / row_total[..., None]).astype(jnp.bfloat16)
    attended = jnp.einsum(
        "qsghbt,qbgtd->qsghd", prefix_p, own_blocks[:, :, 1], preferred_element_type=jnp.float32
    )
    attended = attended + jnp.einsum(
        "qsghj,qjgd->qsghd", fresh_p, fresh_key_value[:, :, 1], preferred_element_type=jnp.float32
    )
    attended = attended.astype(jnp.bfloat16).reshape(req_dev, step_count, query_width)
    base_product = jnp.dot(
        attended.reshape(req_dev * step_count, query_width),
        output_weight,
        preferred_element_type=jnp.float32,
    )
    base_product = base_product.reshape(req_dev, step_count, out_width)
    adapter = request_adapter[:, 0]
    single_panel = lax.all_gather(adapter_down_panels, "dp", axis=0, tiled=True)
    panel_count = single_panel.shape[0]
    hit_mask = (adapter[:, None] == jnp.arange(panel_count)[None, :]).astype(jnp.float32)
    every_rank = jnp.einsum(
        "qsf,nrf->qsnr", attended, single_panel, preferred_element_type=jnp.float32
    )
    rank_part = jnp.einsum("qsnr,qn->qsr", every_rank, hit_mask)
    rank_sum = lax.psum(rank_part, "mp").astype(jnp.bfloat16)
    single_panel = lax.all_gather(adapter_up_panels, "dp", axis=0, tiled=True)
    panel_count = single_panel.shape[0]
    hit_mask = (adapter[:, None] == jnp.arange(panel_count)[None, :]).astype(jnp.bfloat16)
    selected_panel = rank_sum[:, :, None, :] * hit_mask[:, None, :, None]
    adapter_sum = jnp.einsum(
        "utja,jam->utm", selected_panel, single_panel, preferred_element_type=jnp.float32
    )
    adapter_output = (adapter_sum * ADAPTER_SCALE).astype(jnp.bfloat16)
    summed_output = lax.psum_scatter(
        base_product.astype(jnp.bfloat16), "mp", scatter_dimension=2, tiled=True
    )
    return (summed_output + adapter_output.astype(jnp.float32)).astype(jnp.bfloat16)


def solution(mesh):
    in_specs = (
        P("dp", None, "mp"),
        P("dp", None, None, "mp", None),
        P("dp", None, "mp", None, None),
        P(),
        P("dp", None),
        P("dp"),
        P("dp", None),
        P("mp", None),
        P("dp", None, "mp"),
        P("dp", None, "mp"),
    )
    out_specs = P("dp", None, "mp")
    return jax.shard_map(shards, mesh=mesh, in_specs=in_specs, out_specs=out_specs, check_vma=False)
```

```python
import jax
import jax.numpy as jnp
from jax import lax
from jax.sharding import PartitionSpec as P
from jax.experimental import pallas as pl
from jax.experimental.pallas import tpu as pltpu

ADAPTER_SCALE = 2.0


def attention_kernel(idx_ref, rows_ref, q_ref, f_ref, live_ref, out_ref, *, req_blk, blocks_per, token_cap, steps, group, scale):
    i = pl.program_id(0)
    kv_groups, q_rows, _ = q_ref.shape
    cols = live_ref.shape[2]
    prefix_cols = req_blk * token_cap
    fresh_cols = req_blk * steps
    row_id = lax.broadcasted_iota(jnp.int32, (q_rows, cols), 0)
    col_id = lax.broadcasted_iota(jnp.int32, (q_rows, cols), 1)
    row_req = row_id // (steps * group)
    row_step = (row_id % (steps * group)) // group
    fresh_id = col_id - prefix_cols
    col_req = jnp.where(
        col_id < prefix_cols,
        col_id // token_cap,
        jnp.where(fresh_id < fresh_cols, fresh_id // steps, -1),
    )
    step_ok = jnp.logical_or(col_id < prefix_cols, fresh_id % steps <= row_step)
    mask = (col_req == row_req) & step_ok & (live_ref[0] > 0)
    pad_rows = cols - prefix_cols - fresh_cols
    for g in range(kv_groups):
        keys = []
        values = []
        for r in range(req_blk):
            for b in range(blocks_per):
                row = idx_ref[(i * req_blk + r) * blocks_per + b]
                keys.append(rows_ref[row, 0, g])
                values.append(rows_ref[row, 1, g])
        keys.append(f_ref[g, 0])
        values.append(f_ref[g, 1])
        if pad_rows:
            keys.append(jnp.zeros((pad_rows, keys[0].shape[1]), keys[0].dtype))
            values.append(jnp.zeros((pad_rows, values[0].shape[1]), values[0].dtype))
        key_mat = jnp.concatenate(keys, axis=0)
        value_mat = jnp.concatenate(values, axis=0)
        scores = lax.dot_general(
            q_ref[g], key_mat, (((1,), (1,)), ((), ())), preferred_element_type=jnp.float32
        ) * scale
        scores = jnp.where(mask, scores, -jnp.inf)
        top = jnp.max(scores, axis=1, keepdims=True)
        weights = jnp.exp(scores - top)
        total = jnp.sum(weights, axis=1, keepdims=True)
        probs = (weights / total).astype(jnp.bfloat16)
        out_ref[g] = jnp.dot(probs, value_mat, preferred_element_type=jnp.float32).astype(out_ref.dtype)


def attend(row_index, rows, queries, fresh_key_value, live_prefix_length, blocks_per, interpret=False):
    req_dev, steps, _ = queries.shape
    kv_groups = fresh_key_value.shape[3]
    head_dim = fresh_key_value.shape[4]
    block_len = rows.shape[3]
    group = queries.shape[2] // (kv_groups * head_dim)
    token_cap = blocks_per * block_len
    req_blk = 4
    q_rows = req_blk * steps * group
    prefix_cols = req_blk * token_cap
    fresh_cols = req_blk * steps
    cols = -(-(prefix_cols + fresh_cols) // 128) * 128
    q_t = queries.reshape(req_dev, steps, kv_groups, group, head_dim).transpose(2, 0, 1, 3, 4)
    q_t = q_t.reshape(kv_groups, req_dev * steps * group, head_dim)
    f_t = fresh_key_value.transpose(3, 2, 0, 1, 4).reshape(kv_groups, 2, req_dev * steps, head_dim)
    live = (jnp.arange(token_cap)[None, :] < live_prefix_length[:, None]).astype(jnp.int32)
    live = live.reshape(req_dev // req_blk, prefix_cols)
    extra = jnp.concatenate(
        [jnp.ones((fresh_cols,), jnp.int32), jnp.zeros((cols - prefix_cols - fresh_cols,), jnp.int32)]
    )
    live = jnp.concatenate([live, jnp.broadcast_to(extra, (req_dev // req_blk, extra.shape[0]))], axis=1)
    live = live.reshape(req_dev // req_blk, 1, cols)
    body = lambda *refs: attention_kernel(
        *refs, req_blk=req_blk, blocks_per=blocks_per, token_cap=token_cap, steps=steps,
        group=group, scale=head_dim ** (-0.5),
    )
    grid_spec = pltpu.PrefetchScalarGridSpec(
        num_scalar_prefetch=1,
        grid=(req_dev // req_blk,),
        in_specs=[
            pl.BlockSpec(rows.shape, lambda i, idx: (0, 0, 0, 0, 0)),
            pl.BlockSpec((kv_groups, q_rows, head_dim), lambda i, idx: (0, i, 0)),
            pl.BlockSpec((kv_groups, 2, fresh_cols, head_dim), lambda i, idx: (0, 0, i, 0)),
            pl.BlockSpec((1, 1, cols), lambda i, idx: (i, 0, 0)),
        ],
        out_specs=pl.BlockSpec((kv_groups, q_rows, head_dim), lambda i, idx: (0, i, 0)),
    )
    out = pl.pallas_call(
        body,
        grid_spec=grid_spec,
        out_shape=jax.ShapeDtypeStruct(q_t.shape, jnp.bfloat16),
        interpret=interpret,
    )(row_index, rows, q_t, f_t, live)
    out = out.reshape(kv_groups, req_dev, steps, group, head_dim).transpose(1, 2, 0, 3, 4)
    return out.reshape(req_dev, steps, kv_groups * group * head_dim)


def shards(
    queries,
    fresh_key_value,
    key_value_pool,
    block_position_map,
    request_blocks,
    live_prefix_length,
    request_adapter,
    output_weight,
    adapter_down_panels,
    adapter_up_panels,
):
    owners = lax.axis_size("dp")
    req_dev, step_count, query_width = queries.shape
    kv_heads = fresh_key_value.shape[3]
    head_dim = fresh_key_value.shape[4]
    pool_dev = key_value_pool.shape[0]
    block_len = key_value_pool.shape[3]
    blocks_per = request_blocks.shape[1]
    entries = req_dev * blocks_per
    out_width = output_weight.shape[1]
    owner_range = jnp.arange(owners)
    positions = jnp.take(block_position_map, request_blocks.reshape(entries))
    target = positions // pool_dev
    local_slot = positions % pool_dev
    capacity = entries // owners
    entry_ids = jnp.arange(entries)
    same_block = positions[:, None] == positions[None, :]
    earlier = entry_ids[None, :] < entry_ids[:, None]
    first = jnp.logical_not(jnp.any(same_block & earlier, axis=1))
    same_owner = target[:, None] == target[None, :]
    rank = jnp.sum((same_owner & earlier & first[None, :]).astype(jnp.int32), axis=1)
    first_of = same_block & first[None, :]
    slot_index = jnp.sum(jnp.where(first_of, rank[None, :], 0), axis=1)
    key = jnp.where(first, target * capacity + rank, -1)
    table_ids = jnp.arange(owners * capacity)
    wish_table = jnp.sum(
        jnp.where(key[:, None] == table_ids[None, :], local_slot[:, None], 0), axis=0
    ).reshape(owners, capacity)
    wanted = lax.all_to_all(wish_table, "dp", split_axis=0, concat_axis=0, tiled=True)
    served = jnp.take(key_value_pool, wanted.reshape(-1), axis=0).reshape(
        (owners, capacity) + key_value_pool.shape[1:]
    )
    fetched = lax.all_to_all(served, "dp", split_axis=0, concat_axis=0, tiled=True)
    fetched, adapter_down_panels, adapter_up_panels = lax.optimization_barrier(
        (fetched, adapter_down_panels, adapter_up_panels)
    )
    flat_rows = fetched.reshape((owners * capacity,) + key_value_pool.shape[1:])
    row_index = jnp.clip(target * capacity + slot_index, 0, owners * capacity - 1)
    attended = attend(row_index, flat_rows, queries, fresh_key_value, live_prefix_length, blocks_per)
    base_product = jnp.dot(
        attended.reshape(req_dev * step_count, query_width),
        output_weight,
        preferred_element_type=jnp.float32,
    )
    base_product = base_product.reshape(req_dev, step_count, out_width)
    adapter = request_adapter[:, 0]
    single_panel = lax.all_gather(adapter_down_panels, "dp", axis=0, tiled=True)
    panel_count = single_panel.shape[0]
    hit_mask = (adapter[:, None] == jnp.arange(panel_count)[None, :]).astype(jnp.float32)
    every_rank = jnp.einsum(
        "qsf,nrf->qsnr", attended, single_panel, preferred_element_type=jnp.float32
    )
    rank_part = jnp.einsum("qsnr,qn->qsr", every_rank, hit_mask)
    rank_sum = lax.psum(rank_part, "mp").astype(jnp.bfloat16)
    single_panel = lax.all_gather(adapter_up_panels, "dp", axis=0, tiled=True)
    panel_count = single_panel.shape[0]
    hit_mask = (adapter[:, None] == jnp.arange(panel_count)[None, :]).astype(jnp.bfloat16)
    selected_panel = rank_sum[:, :, None, :] * hit_mask[:, None, :, None]
    adapter_sum = jnp.einsum(
        "utja,jam->utm", selected_panel, single_panel, preferred_element_type=jnp.float32
    )
    adapter_output = (adapter_sum * ADAPTER_SCALE).astype(jnp.bfloat16)
    summed_output = lax.psum_scatter(
        base_product.astype(jnp.bfloat16), "mp", scatter_dimension=2, tiled=True
    )
    return (summed_output + adapter_output.astype(jnp.float32)).astype(jnp.bfloat16)


def solution(mesh):
    in_specs = (
        P("dp", None, "mp"),
        P("dp", None, None, "mp", None),
        P("dp", None, "mp", None, None),
        P(),
        P("dp", None),
        P("dp"),
        P("dp", None),
        P("mp", None),
        P("dp", None, "mp"),
        P("dp", None, "mp"),
    )
    out_specs = P("dp", None, "mp")
    return jax.shard_map(shards, mesh=mesh, in_specs=in_specs, out_specs=out_specs, check_vma=False)
```

```python
import jax
import jax.numpy as jnp
from jax import lax
from jax.sharding import PartitionSpec as P
from jax.experimental import pallas as pl
from jax.experimental.pallas import tpu as pltpu

ADAPTER_SCALE = 2.0


def attention_kernel(idx_ref, rows_ref, q_ref, f_ref, live_ref, out_ref, *, req_blk, blocks_per, token_cap, steps, group, scale):
    i = pl.program_id(0)
    kv_groups, q_rows, _ = q_ref.shape
    cols = live_ref.shape[2]
    prefix_cols = req_blk * token_cap
    fresh_cols = req_blk * steps
    row_id = lax.broadcasted_iota(jnp.int32, (q_rows, cols), 0)
    col_id = lax.broadcasted_iota(jnp.int32, (q_rows, cols), 1)
    row_req = row_id // (steps * group)
    row_step = (row_id % (steps * group)) // group
    fresh_id = col_id - prefix_cols
    col_req = jnp.where(
        col_id < prefix_cols,
        col_id // token_cap,
        jnp.where(fresh_id < fresh_cols, fresh_id // steps, -1),
    )
    step_ok = jnp.logical_or(col_id < prefix_cols, fresh_id % steps <= row_step)
    mask = (col_req == row_req) & step_ok & (live_ref[0] > 0)
    pad_rows = cols - prefix_cols - fresh_cols
    for g in range(kv_groups):
        keys = []
        values = []
        for r in range(req_blk):
            for b in range(blocks_per):
                row = idx_ref[(i * req_blk + r) * blocks_per + b]
                keys.append(rows_ref[row, 0, g])
                values.append(rows_ref[row, 1, g])
        keys.append(f_ref[g, 0])
        values.append(f_ref[g, 1])
        if pad_rows:
            keys.append(jnp.zeros((pad_rows, keys[0].shape[1]), keys[0].dtype))
            values.append(jnp.zeros((pad_rows, values[0].shape[1]), values[0].dtype))
        key_mat = jnp.concatenate(keys, axis=0)
        value_mat = jnp.concatenate(values, axis=0)
        scores = lax.dot_general(
            q_ref[g], key_mat, (((1,), (1,)), ((), ())), preferred_element_type=jnp.float32
        ) * scale
        scores = jnp.where(mask, scores, -jnp.inf)
        top = jnp.max(scores, axis=1, keepdims=True)
        weights = jnp.exp(scores - top)
        total = jnp.sum(weights, axis=1, keepdims=True)
        probs = (weights / total).astype(jnp.bfloat16)
        out_ref[g] = jnp.dot(probs, value_mat, preferred_element_type=jnp.float32).astype(out_ref.dtype)


def attend(row_index, rows, queries, fresh_key_value, live_prefix_length, blocks_per, interpret=False):
    req_dev, steps, _ = queries.shape
    kv_groups = fresh_key_value.shape[3]
    head_dim = fresh_key_value.shape[4]
    block_len = rows.shape[3]
    group = queries.shape[2] // (kv_groups * head_dim)
    token_cap = blocks_per * block_len
    req_blk = 4
    q_rows = req_blk * steps * group
    prefix_cols = req_blk * token_cap
    fresh_cols = req_blk * steps
    cols = -(-(prefix_cols + fresh_cols) // 128) * 128
    q_t = queries.reshape(req_dev, steps, kv_groups, group, head_dim).transpose(2, 0, 1, 3, 4)
    q_t = q_t.reshape(kv_groups, req_dev * steps * group, head_dim)
    f_t = fresh_key_value.transpose(3, 2, 0, 1, 4).reshape(kv_groups, 2, req_dev * steps, head_dim)
    live = (jnp.arange(token_cap)[None, :] < live_prefix_length[:, None]).astype(jnp.int32)
    live = live.reshape(req_dev // req_blk, prefix_cols)
    extra = jnp.concatenate(
        [jnp.ones((fresh_cols,), jnp.int32), jnp.zeros((cols - prefix_cols - fresh_cols,), jnp.int32)]
    )
    live = jnp.concatenate([live, jnp.broadcast_to(extra, (req_dev // req_blk, extra.shape[0]))], axis=1)
    live = live.reshape(req_dev // req_blk, 1, cols)
    body = lambda *refs: attention_kernel(
        *refs, req_blk=req_blk, blocks_per=blocks_per, token_cap=token_cap, steps=steps,
        group=group, scale=head_dim ** (-0.5),
    )
    grid_spec = pltpu.PrefetchScalarGridSpec(
        num_scalar_prefetch=1,
        grid=(req_dev // req_blk,),
        in_specs=[
            pl.BlockSpec(rows.shape, lambda i, idx: (0, 0, 0, 0, 0)),
            pl.BlockSpec((kv_groups, q_rows, head_dim), lambda i, idx: (0, i, 0)),
            pl.BlockSpec((kv_groups, 2, fresh_cols, head_dim), lambda i, idx: (0, 0, i, 0)),
            pl.BlockSpec((1, 1, cols), lambda i, idx: (i, 0, 0)),
        ],
        out_specs=pl.BlockSpec((kv_groups, q_rows, head_dim), lambda i, idx: (0, i, 0)),
    )
    out = pl.pallas_call(
        body,
        grid_spec=grid_spec,
        out_shape=jax.ShapeDtypeStruct(q_t.shape, jnp.bfloat16),
        interpret=interpret,
    )(row_index, rows, q_t, f_t, live)
    out = out.reshape(kv_groups, req_dev, steps, group, head_dim).transpose(1, 2, 0, 3, 4)
    return out.reshape(req_dev, steps, kv_groups * group * head_dim)


def shards(
    queries,
    fresh_key_value,
    key_value_pool,
    block_position_map,
    request_blocks,
    live_prefix_length,
    request_adapter,
    output_weight,
    adapter_down_panels,
    adapter_up_panels,
):
    owners = lax.axis_size("dp")
    req_dev, step_count, query_width = queries.shape
    kv_heads = fresh_key_value.shape[3]
    head_dim = fresh_key_value.shape[4]
    pool_dev = key_value_pool.shape[0]
    block_len = key_value_pool.shape[3]
    blocks_per = request_blocks.shape[1]
    entries = req_dev * blocks_per
    out_width = output_weight.shape[1]
    owner_range = jnp.arange(owners)
    positions = jnp.take(block_position_map, request_blocks.reshape(entries))
    target = positions // pool_dev
    local_slot = positions % pool_dev
    capacity = entries // owners
    entry_ids = jnp.arange(entries)
    same_block = positions[:, None] == positions[None, :]
    earlier = entry_ids[None, :] < entry_ids[:, None]
    first = jnp.logical_not(jnp.any(same_block & earlier, axis=1))
    same_owner = target[:, None] == target[None, :]
    rank = jnp.sum((same_owner & earlier & first[None, :]).astype(jnp.int32), axis=1)
    first_of = same_block & first[None, :]
    slot_index = jnp.sum(jnp.where(first_of, rank[None, :], 0), axis=1)
    key = jnp.where(first, target * capacity + rank, -1)
    table_ids = jnp.arange(owners * capacity)
    wish_table = jnp.sum(
        jnp.where(key[:, None] == table_ids[None, :], local_slot[:, None], 0), axis=0
    ).reshape(owners, capacity)
    wanted = lax.all_to_all(wish_table, "dp", split_axis=0, concat_axis=0, tiled=True)
    served = jnp.take(key_value_pool, wanted.reshape(-1), axis=0, mode="clip").reshape(
        (owners, capacity) + key_value_pool.shape[1:]
    )
    fetched = lax.all_to_all(served, "dp", split_axis=0, concat_axis=0, tiled=True)
    fetched, adapter_up_panels = lax.optimization_barrier((fetched, adapter_up_panels))
    flat_rows = fetched.reshape((owners * capacity,) + key_value_pool.shape[1:])
    row_index = jnp.clip(target * capacity + slot_index, 0, owners * capacity - 1)
    attended = attend(row_index, flat_rows, queries, fresh_key_value, live_prefix_length, blocks_per)
    base_product = jnp.dot(
        attended.reshape(req_dev * step_count, query_width),
        output_weight,
        preferred_element_type=jnp.float32,
    )
    base_product = base_product.reshape(req_dev, step_count, out_width)
    adapter = request_adapter[:, 0]
    single_panel = lax.all_gather(adapter_down_panels, "dp", axis=0, tiled=True)
    panel_count = single_panel.shape[0]
    hit_mask = (adapter[:, None] == jnp.arange(panel_count)[None, :]).astype(jnp.float32)
    every_rank = jnp.einsum(
        "qsf,nrf->qsnr", attended, single_panel, preferred_element_type=jnp.float32
    )
    rank_part = jnp.einsum("qsnr,qn->qsr", every_rank, hit_mask)
    rank_sum = lax.psum(rank_part, "mp").astype(jnp.bfloat16)
    single_panel = lax.all_gather(adapter_up_panels, "dp", axis=0, tiled=True)
    panel_count = single_panel.shape[0]
    hit_mask = (adapter[:, None] == jnp.arange(panel_count)[None, :]).astype(jnp.bfloat16)
    selected_panel = rank_sum[:, :, None, :] * hit_mask[:, None, :, None]
    adapter_sum = jnp.einsum(
        "utja,jam->utm", selected_panel, single_panel, preferred_element_type=jnp.float32
    )
    adapter_output = (adapter_sum * ADAPTER_SCALE).astype(jnp.bfloat16)
    summed_output = lax.psum_scatter(
        base_product.astype(jnp.bfloat16), "mp", scatter_dimension=2, tiled=True
    )
    return (summed_output + adapter_output.astype(jnp.float32)).astype(jnp.bfloat16)


def solution(mesh):
    in_specs = (
        P("dp", None, "mp"),
        P("dp", None, None, "mp", None),
        P("dp", None, "mp", None, None),
        P(),
        P("dp", None),
        P("dp"),
        P("dp", None),
        P("mp", None),
        P("dp", None, "mp"),
        P("dp", None, "mp"),
    )
    out_specs = P("dp", None, "mp")
    return jax.shard_map(shards, mesh=mesh, in_specs=in_specs, out_specs=out_specs, check_vma=False)
```

```python
import jax
import jax.numpy as jnp
from jax import lax
from jax.sharding import PartitionSpec as P
from jax.experimental import pallas as pl
from jax.experimental.pallas import tpu as pltpu

ADAPTER_SCALE = 2.0
ADAPTER_CAP = 8


def attention_kernel(idx_ref, rows_ref, q_ref, f_ref, live_ref, out_ref, *, req_blk, blocks_per, token_cap, steps, group, scale):
    i = pl.program_id(0)
    kv_groups, q_rows, _ = q_ref.shape
    cols = live_ref.shape[2]
    prefix_cols = req_blk * token_cap
    fresh_cols = req_blk * steps
    row_id = lax.broadcasted_iota(jnp.int32, (q_rows, cols), 0)
    col_id = lax.broadcasted_iota(jnp.int32, (q_rows, cols), 1)
    row_req = row_id // (steps * group)
    row_step = (row_id % (steps * group)) // group
    fresh_id = col_id - prefix_cols
    col_req = jnp.where(
        col_id < prefix_cols,
        col_id // token_cap,
        jnp.where(fresh_id < fresh_cols, fresh_id // steps, -1),
    )
    step_ok = jnp.logical_or(col_id < prefix_cols, fresh_id % steps <= row_step)
    mask = (col_req == row_req) & step_ok & (live_ref[0] > 0)
    pad_rows = cols - prefix_cols - fresh_cols
    for g in range(kv_groups):
        keys = []
        values = []
        for r in range(req_blk):
            for b in range(blocks_per):
                row = idx_ref[(i * req_blk + r) * blocks_per + b]
                keys.append(rows_ref[row, 0, g])
                values.append(rows_ref[row, 1, g])
        keys.append(f_ref[g, 0])
        values.append(f_ref[g, 1])
        if pad_rows:
            keys.append(jnp.zeros((pad_rows, keys[0].shape[1]), keys[0].dtype))
            values.append(jnp.zeros((pad_rows, values[0].shape[1]), values[0].dtype))
        key_mat = jnp.concatenate(keys, axis=0)
        value_mat = jnp.concatenate(values, axis=0)
        scores = lax.dot_general(
            q_ref[g], key_mat, (((1,), (1,)), ((), ())), preferred_element_type=jnp.float32
        ) * scale
        scores = jnp.where(mask, scores, -jnp.inf)
        top = jnp.max(scores, axis=1, keepdims=True)
        weights = jnp.exp(scores - top)
        total = jnp.sum(weights, axis=1, keepdims=True)
        probs = (weights / total).astype(jnp.bfloat16)
        out_ref[g] = jnp.dot(probs, value_mat, preferred_element_type=jnp.float32).astype(out_ref.dtype)


def attend(row_index, rows, queries, fresh_key_value, live_prefix_length, blocks_per, interpret=False):
    req_dev, steps, _ = queries.shape
    kv_groups = fresh_key_value.shape[3]
    head_dim = fresh_key_value.shape[4]
    block_len = rows.shape[3]
    group = queries.shape[2] // (kv_groups * head_dim)
    token_cap = blocks_per * block_len
    req_blk = 4
    q_rows = req_blk * steps * group
    prefix_cols = req_blk * token_cap
    fresh_cols = req_blk * steps
    cols = -(-(prefix_cols + fresh_cols) // 128) * 128
    q_t = queries.reshape(req_dev, steps, kv_groups, group, head_dim).transpose(2, 0, 1, 3, 4)
    q_t = q_t.reshape(kv_groups, req_dev * steps * group, head_dim)
    f_t = fresh_key_value.transpose(3, 2, 0, 1, 4).reshape(kv_groups, 2, req_dev * steps, head_dim)
    live = (jnp.arange(token_cap)[None, :] < live_prefix_length[:, None]).astype(jnp.int32)
    live = live.reshape(req_dev // req_blk, prefix_cols)
    extra = jnp.concatenate(
        [jnp.ones((fresh_cols,), jnp.int32), jnp.zeros((cols - prefix_cols - fresh_cols,), jnp.int32)]
    )
    live = jnp.concatenate([live, jnp.broadcast_to(extra, (req_dev // req_blk, extra.shape[0]))], axis=1)
    live = live.reshape(req_dev // req_blk, 1, cols)
    body = lambda *refs: attention_kernel(
        *refs, req_blk=req_blk, blocks_per=blocks_per, token_cap=token_cap, steps=steps,
        group=group, scale=head_dim ** (-0.5),
    )
    grid_spec = pltpu.PrefetchScalarGridSpec(
        num_scalar_prefetch=1,
        grid=(req_dev // req_blk,),
        in_specs=[
            pl.BlockSpec(rows.shape, lambda i, idx: (0, 0, 0, 0, 0)),
            pl.BlockSpec((kv_groups, q_rows, head_dim), lambda i, idx: (0, i, 0)),
            pl.BlockSpec((kv_groups, 2, fresh_cols, head_dim), lambda i, idx: (0, 0, i, 0)),
            pl.BlockSpec((1, 1, cols), lambda i, idx: (i, 0, 0)),
        ],
        out_specs=pl.BlockSpec((kv_groups, q_rows, head_dim), lambda i, idx: (0, i, 0)),
    )
    out = pl.pallas_call(
        body,
        grid_spec=grid_spec,
        out_shape=jax.ShapeDtypeStruct(q_t.shape, jnp.bfloat16),
        interpret=interpret,
    )(row_index, rows, q_t, f_t, live)
    out = out.reshape(kv_groups, req_dev, steps, group, head_dim).transpose(1, 2, 0, 3, 4)
    return out.reshape(req_dev, steps, kv_groups * group * head_dim)


def shards(
    queries,
    fresh_key_value,
    key_value_pool,
    block_position_map,
    request_blocks,
    live_prefix_length,
    request_adapter,
    output_weight,
    adapter_down_panels,
    adapter_up_panels,
):
    owners = lax.axis_size("dp")
    req_dev, step_count, query_width = queries.shape
    kv_heads = fresh_key_value.shape[3]
    head_dim = fresh_key_value.shape[4]
    pool_dev = key_value_pool.shape[0]
    block_len = key_value_pool.shape[3]
    blocks_per = request_blocks.shape[1]
    entries = req_dev * blocks_per
    out_width = output_weight.shape[1]
    owner_range = jnp.arange(owners)
    positions = jnp.take(block_position_map, request_blocks.reshape(entries))
    target = positions // pool_dev
    local_slot = positions % pool_dev
    capacity = entries // owners
    entry_ids = jnp.arange(entries)
    same_block = positions[:, None] == positions[None, :]
    earlier = entry_ids[None, :] < entry_ids[:, None]
    first = jnp.logical_not(jnp.any(same_block & earlier, axis=1))
    same_owner = target[:, None] == target[None, :]
    rank = jnp.sum((same_owner & earlier & first[None, :]).astype(jnp.int32), axis=1)
    first_of = same_block & first[None, :]
    slot_index = jnp.sum(jnp.where(first_of, rank[None, :], 0), axis=1)
    key = jnp.where(first, target * capacity + rank, -1)
    table_ids = jnp.arange(owners * capacity)
    wish_table = jnp.sum(
        jnp.where(key[:, None] == table_ids[None, :], local_slot[:, None], 0), axis=0
    ).reshape(owners, capacity)
    wanted = lax.all_to_all(wish_table, "dp", split_axis=0, concat_axis=0, tiled=True)
    served = jnp.take(key_value_pool, wanted.reshape(-1), axis=0, mode="clip").reshape(
        (owners, capacity) + key_value_pool.shape[1:]
    )
    fetched = lax.all_to_all(served, "dp", split_axis=0, concat_axis=0, tiled=True)
    flat_rows = fetched.reshape((owners * capacity,) + key_value_pool.shape[1:])
    row_index = jnp.clip(target * capacity + slot_index, 0, owners * capacity - 1)
    attended = attend(row_index, flat_rows, queries, fresh_key_value, live_prefix_length, blocks_per)
    base_product = jnp.dot(
        attended.reshape(req_dev * step_count, query_width),
        output_weight,
        preferred_element_type=jnp.float32,
    )
    base_product = base_product.reshape(req_dev, step_count, out_width)
    adapter = request_adapter[:, 0]
    local_adapters, rank_dim, _ = adapter_down_panels.shape
    slots = local_adapters * ADAPTER_CAP
    request_ids = jnp.arange(req_dev)
    same_adapter = adapter[:, None] == adapter[None, :]
    before = request_ids[None, :] < request_ids[:, None]
    repeat = jnp.sum((same_adapter & before).astype(jnp.int32), axis=1)
    flat_slot = (adapter // local_adapters) * slots + (adapter % local_adapters) * ADAPTER_CAP + repeat
    slot_ids = jnp.arange(owners * slots)
    slot_owner = jnp.sum(
        jnp.where(flat_slot[:, None] == slot_ids[None, :], request_ids[:, None], 0), axis=0
    )
    outgoing = jnp.take(attended, slot_owner, axis=0, mode="clip")
    incoming = lax.all_to_all(
        outgoing.reshape((owners, slots) + attended.shape[1:]), "dp", split_axis=0, concat_axis=0, tiled=True
    )
    incoming = incoming.reshape(owners, local_adapters, ADAPTER_CAP, step_count, -1)
    rank_part = jnp.einsum(
        "onksf,nrf->onksr", incoming, adapter_down_panels, preferred_element_type=jnp.float32
    )
    rank_sum = lax.psum(rank_part, "mp").astype(jnp.bfloat16)
    adapter_sum = jnp.einsum(
        "onksr,nrm->onksm", rank_sum, adapter_up_panels, preferred_element_type=jnp.float32
    )
    adapter_rows = (adapter_sum * ADAPTER_SCALE).astype(jnp.bfloat16)
    returned = lax.all_to_all(
        adapter_rows.reshape(owners, slots, step_count, -1), "dp", split_axis=0, concat_axis=0, tiled=True
    )
    returned = returned.reshape(owners * slots, step_count, -1)
    adapter_output = jnp.take(returned, jnp.clip(flat_slot, 0, owners * slots - 1), axis=0, mode="clip")
    summed_output = lax.psum_scatter(
        base_product.astype(jnp.bfloat16), "mp", scatter_dimension=2, tiled=True
    )
    return (summed_output + adapter_output.astype(jnp.float32)).astype(jnp.bfloat16)


def solution(mesh):
    in_specs = (
        P("dp", None, "mp"),
        P("dp", None, None, "mp", None),
        P("dp", None, "mp", None, None),
        P(),
        P("dp", None),
        P("dp"),
        P("dp", None),
        P("mp", None),
        P("dp", None, "mp"),
        P("dp", None, "mp"),
    )
    out_specs = P("dp", None, "mp")
    return jax.shard_map(shards, mesh=mesh, in_specs=in_specs, out_specs=out_specs, check_vma=False)
```

```python
import jax
import jax.numpy as jnp
from jax import lax
from jax.sharding import PartitionSpec as P
from jax.experimental import pallas as pl
from jax.experimental.pallas import tpu as pltpu

ADAPTER_SCALE = 2.0


def gather_rows_kernel(idx_ref, src_ref, dst_ref, sems):
    count = dst_ref.shape[0]
    depth = sems.shape[0]

    def copy(j):
        return pltpu.make_async_copy(src_ref.at[idx_ref[j]], dst_ref.at[j], sems.at[j % depth])

    def issue(j, carry):
        @pl.when(j >= depth)
        def _():
            copy(j - depth).wait()

        copy(j).start()
        return carry

    def drain(j, carry):
        copy(j).wait()
        return carry

    lax.fori_loop(0, count, issue, 0)
    lax.fori_loop(count - depth, count, drain, 0)


def gather_rows(table, index, interpret=False):
    count = index.shape[0]
    depth = min(16, count)
    grid_spec = pltpu.PrefetchScalarGridSpec(
        num_scalar_prefetch=1,
        grid=(1,),
        in_specs=[pl.BlockSpec(memory_space=pl.ANY)],
        out_specs=pl.BlockSpec(memory_space=pl.ANY),
        scratch_shapes=[pltpu.SemaphoreType.DMA((depth,))],
    )
    return pl.pallas_call(
        gather_rows_kernel,
        grid_spec=grid_spec,
        out_shape=jax.ShapeDtypeStruct((count,) + table.shape[1:], table.dtype),
        interpret=interpret,
    )(index, table)


def attention_kernel(idx_ref, rows_ref, q_ref, f_ref, live_ref, out_ref, *, req_blk, blocks_per, token_cap, steps, group, scale):
    i = pl.program_id(0)
    kv_groups, q_rows, _ = q_ref.shape
    cols = live_ref.shape[2]
    prefix_cols = req_blk * token_cap
    fresh_cols = req_blk * steps
    row_id = lax.broadcasted_iota(jnp.int32, (q_rows, cols), 0)
    col_id = lax.broadcasted_iota(jnp.int32, (q_rows, cols), 1)
    row_req = row_id // (steps * group)
    row_step = (row_id % (steps * group)) // group
    fresh_id = col_id - prefix_cols
    col_req = jnp.where(
        col_id < prefix_cols,
        col_id // token_cap,
        jnp.where(fresh_id < fresh_cols, fresh_id // steps, -1),
    )
    step_ok = jnp.logical_or(col_id < prefix_cols, fresh_id % steps <= row_step)
    mask = (col_req == row_req) & step_ok & (live_ref[0] > 0)
    pad_rows = cols - prefix_cols - fresh_cols
    for g in range(kv_groups):
        keys = []
        values = []
        for r in range(req_blk):
            for b in range(blocks_per):
                row = idx_ref[(i * req_blk + r) * blocks_per + b]
                keys.append(rows_ref[row, 0, g])
                values.append(rows_ref[row, 1, g])
        keys.append(f_ref[g, 0])
        values.append(f_ref[g, 1])
        if pad_rows:
            keys.append(jnp.zeros((pad_rows, keys[0].shape[1]), keys[0].dtype))
            values.append(jnp.zeros((pad_rows, values[0].shape[1]), values[0].dtype))
        key_mat = jnp.concatenate(keys, axis=0)
        value_mat = jnp.concatenate(values, axis=0)
        scores = lax.dot_general(
            q_ref[g], key_mat, (((1,), (1,)), ((), ())), preferred_element_type=jnp.float32
        ) * scale
        scores = jnp.where(mask, scores, -jnp.inf)
        top = jnp.max(scores, axis=1, keepdims=True)
        weights = jnp.exp(scores - top)
        total = jnp.sum(weights, axis=1, keepdims=True)
        probs = (weights / total).astype(jnp.bfloat16)
        out_ref[g] = jnp.dot(probs, value_mat, preferred_element_type=jnp.float32).astype(out_ref.dtype)


def attend(row_index, rows, queries, fresh_key_value, live_prefix_length, blocks_per, interpret=False):
    req_dev, steps, _ = queries.shape
    kv_groups = fresh_key_value.shape[3]
    head_dim = fresh_key_value.shape[4]
    block_len = rows.shape[3]
    group = queries.shape[2] // (kv_groups * head_dim)
    token_cap = blocks_per * block_len
    req_blk = 4
    q_rows = req_blk * steps * group
    prefix_cols = req_blk * token_cap
    fresh_cols = req_blk * steps
    cols = -(-(prefix_cols + fresh_cols) // 128) * 128
    q_t = queries.reshape(req_dev, steps, kv_groups, group, head_dim).transpose(2, 0, 1, 3, 4)
    q_t = q_t.reshape(kv_groups, req_dev * steps * group, head_dim)
    f_t = fresh_key_value.transpose(3, 2, 0, 1, 4).reshape(kv_groups, 2, req_dev * steps, head_dim)
    live = (jnp.arange(token_cap)[None, :] < live_prefix_length[:, None]).astype(jnp.int32)
    live = live.reshape(req_dev // req_blk, prefix_cols)
    extra = jnp.concatenate(
        [jnp.ones((fresh_cols,), jnp.int32), jnp.zeros((cols - prefix_cols - fresh_cols,), jnp.int32)]
    )
    live = jnp.concatenate([live, jnp.broadcast_to(extra, (req_dev // req_blk, extra.shape[0]))], axis=1)
    live = live.reshape(req_dev // req_blk, 1, cols)
    body = lambda *refs: attention_kernel(
        *refs, req_blk=req_blk, blocks_per=blocks_per, token_cap=token_cap, steps=steps,
        group=group, scale=head_dim ** (-0.5),
    )
    grid_spec = pltpu.PrefetchScalarGridSpec(
        num_scalar_prefetch=1,
        grid=(req_dev // req_blk,),
        in_specs=[
            pl.BlockSpec(rows.shape, lambda i, idx: (0, 0, 0, 0, 0)),
            pl.BlockSpec((kv_groups, q_rows, head_dim), lambda i, idx: (0, i, 0)),
            pl.BlockSpec((kv_groups, 2, fresh_cols, head_dim), lambda i, idx: (0, 0, i, 0)),
            pl.BlockSpec((1, 1, cols), lambda i, idx: (i, 0, 0)),
        ],
        out_specs=pl.BlockSpec((kv_groups, q_rows, head_dim), lambda i, idx: (0, i, 0)),
    )
    out = pl.pallas_call(
        body,
        grid_spec=grid_spec,
        out_shape=jax.ShapeDtypeStruct(q_t.shape, jnp.bfloat16),
        interpret=interpret,
    )(row_index, rows, q_t, f_t, live)
    out = out.reshape(kv_groups, req_dev, steps, group, head_dim).transpose(1, 2, 0, 3, 4)
    return out.reshape(req_dev, steps, kv_groups * group * head_dim)


def shards(
    queries,
    fresh_key_value,
    key_value_pool,
    block_position_map,
    request_blocks,
    live_prefix_length,
    request_adapter,
    output_weight,
    adapter_down_panels,
    adapter_up_panels,
):
    owners = lax.axis_size("dp")
    req_dev, step_count, query_width = queries.shape
    kv_heads = fresh_key_value.shape[3]
    head_dim = fresh_key_value.shape[4]
    pool_dev = key_value_pool.shape[0]
    block_len = key_value_pool.shape[3]
    blocks_per = request_blocks.shape[1]
    entries = req_dev * blocks_per
    out_width = output_weight.shape[1]
    owner_range = jnp.arange(owners)
    positions = jnp.take(block_position_map, request_blocks.reshape(entries))
    target = positions // pool_dev
    local_slot = positions % pool_dev
    capacity = entries // owners
    entry_ids = jnp.arange(entries)
    same_block = positions[:, None] == positions[None, :]
    earlier = entry_ids[None, :] < entry_ids[:, None]
    first = jnp.logical_not(jnp.any(same_block & earlier, axis=1))
    same_owner = target[:, None] == target[None, :]
    rank = jnp.sum((same_owner & earlier & first[None, :]).astype(jnp.int32), axis=1)
    first_of = same_block & first[None, :]
    slot_index = jnp.sum(jnp.where(first_of, rank[None, :], 0), axis=1)
    key = jnp.where(first, target * capacity + rank, -1)
    table_ids = jnp.arange(owners * capacity)
    wish_table = jnp.sum(
        jnp.where(key[:, None] == table_ids[None, :], local_slot[:, None], 0), axis=0
    ).reshape(owners, capacity)
    wanted = lax.all_to_all(wish_table, "dp", split_axis=0, concat_axis=0, tiled=True)
    served = gather_rows(key_value_pool, jnp.clip(wanted.reshape(-1), 0, pool_dev - 1)).reshape(
        (owners, capacity) + key_value_pool.shape[1:]
    )
    fetched = lax.all_to_all(served, "dp", split_axis=0, concat_axis=0, tiled=True)
    fetched, adapter_down_panels, adapter_up_panels = lax.optimization_barrier(
        (fetched, adapter_down_panels, adapter_up_panels)
    )
    flat_rows = fetched.reshape((owners * capacity,) + key_value_pool.shape[1:])
    row_index = jnp.clip(target * capacity + slot_index, 0, owners * capacity - 1)
    attended = attend(row_index, flat_rows, queries, fresh_key_value, live_prefix_length, blocks_per)
    base_product = jnp.dot(
        attended.reshape(req_dev * step_count, query_width),
        output_weight,
        preferred_element_type=jnp.float32,
    )
    base_product = base_product.reshape(req_dev, step_count, out_width)
    adapter = request_adapter[:, 0]
    single_panel = lax.all_gather(adapter_down_panels, "dp", axis=0, tiled=True)
    panel_count = single_panel.shape[0]
    hit_mask = (adapter[:, None] == jnp.arange(panel_count)[None, :]).astype(jnp.float32)
    every_rank = jnp.einsum(
        "qsf,nrf->qsnr", attended, single_panel, preferred_element_type=jnp.float32
    )
    rank_part = jnp.einsum("qsnr,qn->qsr", every_rank, hit_mask)
    rank_sum = lax.psum(rank_part, "mp").astype(jnp.bfloat16)
    single_panel = lax.all_gather(adapter_up_panels, "dp", axis=0, tiled=True)
    panel_count = single_panel.shape[0]
    hit_mask = (adapter[:, None] == jnp.arange(panel_count)[None, :]).astype(jnp.bfloat16)
    selected_panel = rank_sum[:, :, None, :] * hit_mask[:, None, :, None]
    adapter_sum = jnp.einsum(
        "utja,jam->utm", selected_panel, single_panel, preferred_element_type=jnp.float32
    )
    adapter_output = (adapter_sum * ADAPTER_SCALE).astype(jnp.bfloat16)
    summed_output = lax.psum_scatter(
        base_product.astype(jnp.bfloat16), "mp", scatter_dimension=2, tiled=True
    )
    return (summed_output + adapter_output.astype(jnp.float32)).astype(jnp.bfloat16)


def solution(mesh):
    in_specs = (
        P("dp", None, "mp"),
        P("dp", None, None, "mp", None),
        P("dp", None, "mp", None, None),
        P(),
        P("dp", None),
        P("dp"),
        P("dp", None),
        P("mp", None),
        P("dp", None, "mp"),
        P("dp", None, "mp"),
    )
    out_specs = P("dp", None, "mp")
    return jax.shard_map(shards, mesh=mesh, in_specs=in_specs, out_specs=out_specs, check_vma=False)
```

```python
import jax
import jax.numpy as jnp
from jax import lax
from jax.sharding import PartitionSpec as P
from jax.experimental import pallas as pl
from jax.experimental.pallas import tpu as pltpu

ADAPTER_SCALE = 2.0


def attention_kernel(idx_ref, rows_ref, q_ref, f_ref, live_ref, out_ref, *, req_blk, blocks_per, token_cap, steps, group, scale):
    i = pl.program_id(0)
    kv_groups, q_rows, _ = q_ref.shape
    cols = live_ref.shape[2]
    prefix_cols = req_blk * token_cap
    fresh_cols = req_blk * steps
    row_id = lax.broadcasted_iota(jnp.int32, (q_rows, cols), 0)
    col_id = lax.broadcasted_iota(jnp.int32, (q_rows, cols), 1)
    row_req = row_id // (steps * group)
    row_step = (row_id % (steps * group)) // group
    fresh_id = col_id - prefix_cols
    col_req = jnp.where(
        col_id < prefix_cols,
        col_id // token_cap,
        jnp.where(fresh_id < fresh_cols, fresh_id // steps, -1),
    )
    step_ok = jnp.logical_or(col_id < prefix_cols, fresh_id % steps <= row_step)
    mask = (col_req == row_req) & step_ok & (live_ref[0] > 0)
    pad_rows = cols - prefix_cols - fresh_cols
    for g in range(kv_groups):
        keys = []
        values = []
        for r in range(req_blk):
            for b in range(blocks_per):
                row = idx_ref[(i * req_blk + r) * blocks_per + b]
                keys.append(rows_ref[row, 0, g])
                values.append(rows_ref[row, 1, g])
        keys.append(f_ref[g, 0])
        values.append(f_ref[g, 1])
        if pad_rows:
            keys.append(jnp.zeros((pad_rows, keys[0].shape[1]), keys[0].dtype))
            values.append(jnp.zeros((pad_rows, values[0].shape[1]), values[0].dtype))
        key_mat = jnp.concatenate(keys, axis=0)
        value_mat = jnp.concatenate(values, axis=0)
        scores = lax.dot_general(
            q_ref[g], key_mat, (((1,), (1,)), ((), ())), preferred_element_type=jnp.float32
        ) * scale
        scores = jnp.where(mask, scores, -jnp.inf)
        top = jnp.max(scores, axis=1, keepdims=True)
        weights = jnp.exp(scores - top)
        total = jnp.sum(weights, axis=1, keepdims=True)
        probs = (weights / total).astype(jnp.bfloat16)
        out_ref[g] = jnp.dot(probs, value_mat, preferred_element_type=jnp.float32).astype(out_ref.dtype)


def attend(row_index, rows, queries, fresh_key_value, live_prefix_length, blocks_per, interpret=False):
    req_dev, steps, _ = queries.shape
    kv_groups = fresh_key_value.shape[3]
    head_dim = fresh_key_value.shape[4]
    block_len = rows.shape[3]
    group = queries.shape[2] // (kv_groups * head_dim)
    token_cap = blocks_per * block_len
    req_blk = 4
    q_rows = req_blk * steps * group
    prefix_cols = req_blk * token_cap
    fresh_cols = req_blk * steps
    cols = -(-(prefix_cols + fresh_cols) // 128) * 128
    q_t = queries.reshape(req_dev, steps, kv_groups, group, head_dim).transpose(2, 0, 1, 3, 4)
    q_t = q_t.reshape(kv_groups, req_dev * steps * group, head_dim)
    f_t = fresh_key_value.transpose(3, 2, 0, 1, 4).reshape(kv_groups, 2, req_dev * steps, head_dim)
    live = (jnp.arange(token_cap)[None, :] < live_prefix_length[:, None]).astype(jnp.int32)
    live = live.reshape(req_dev // req_blk, prefix_cols)
    extra = jnp.concatenate(
        [jnp.ones((fresh_cols,), jnp.int32), jnp.zeros((cols - prefix_cols - fresh_cols,), jnp.int32)]
    )
    live = jnp.concatenate([live, jnp.broadcast_to(extra, (req_dev // req_blk, extra.shape[0]))], axis=1)
    live = live.reshape(req_dev // req_blk, 1, cols)
    body = lambda *refs: attention_kernel(
        *refs, req_blk=req_blk, blocks_per=blocks_per, token_cap=token_cap, steps=steps,
        group=group, scale=head_dim ** (-0.5),
    )
    grid_spec = pltpu.PrefetchScalarGridSpec(
        num_scalar_prefetch=1,
        grid=(req_dev // req_blk,),
        in_specs=[
            pl.BlockSpec(rows.shape, lambda i, idx: (0, 0, 0, 0, 0)),
            pl.BlockSpec((kv_groups, q_rows, head_dim), lambda i, idx: (0, i, 0)),
            pl.BlockSpec((kv_groups, 2, fresh_cols, head_dim), lambda i, idx: (0, 0, i, 0)),
            pl.BlockSpec((1, 1, cols), lambda i, idx: (i, 0, 0)),
        ],
        out_specs=pl.BlockSpec((kv_groups, q_rows, head_dim), lambda i, idx: (0, i, 0)),
    )
    out = pl.pallas_call(
        body,
        grid_spec=grid_spec,
        out_shape=jax.ShapeDtypeStruct(q_t.shape, jnp.bfloat16),
        interpret=interpret,
    )(row_index, rows, q_t, f_t, live)
    out = out.reshape(kv_groups, req_dev, steps, group, head_dim).transpose(1, 2, 0, 3, 4)
    return out.reshape(req_dev, steps, kv_groups * group * head_dim)


def shards(
    queries,
    fresh_key_value,
    key_value_pool,
    block_position_map,
    request_blocks,
    live_prefix_length,
    request_adapter,
    output_weight,
    adapter_down_panels,
    adapter_up_panels,
):
    owners = lax.axis_size("dp")
    req_dev, step_count, query_width = queries.shape
    kv_heads = fresh_key_value.shape[3]
    head_dim = fresh_key_value.shape[4]
    pool_dev = key_value_pool.shape[0]
    block_len = key_value_pool.shape[3]
    blocks_per = request_blocks.shape[1]
    entries = req_dev * blocks_per
    out_width = output_weight.shape[1]
    owner_range = jnp.arange(owners)
    positions = jnp.take(block_position_map, request_blocks.reshape(entries))
    target = positions // pool_dev
    local_slot = positions % pool_dev
    capacity = entries // owners
    entry_ids = jnp.arange(entries)
    same_block = positions[:, None] == positions[None, :]
    earlier = entry_ids[None, :] < entry_ids[:, None]
    first = jnp.logical_not(jnp.any(same_block & earlier, axis=1))
    same_owner = target[:, None] == target[None, :]
    rank = jnp.sum((same_owner & earlier & first[None, :]).astype(jnp.int32), axis=1)
    first_of = same_block & first[None, :]
    slot_index = jnp.sum(jnp.where(first_of, rank[None, :], 0), axis=1)
    key = jnp.where(first, target * capacity + rank, -1)
    table_ids = jnp.arange(owners * capacity)
    wish_table = jnp.sum(
        jnp.where(key[:, None] == table_ids[None, :], local_slot[:, None], 0), axis=0
    ).reshape(owners, capacity)
    wanted = lax.all_to_all(wish_table, "dp", split_axis=0, concat_axis=0, tiled=True)
    pick = (wanted.reshape(-1)[:, None] == jnp.arange(pool_dev)[None, :]).astype(key_value_pool.dtype)
    served = jnp.dot(
        pick, key_value_pool.reshape(pool_dev, -1), preferred_element_type=jnp.float32
    ).astype(key_value_pool.dtype).reshape(
        (owners, capacity) + key_value_pool.shape[1:]
    )
    fetched = lax.all_to_all(served, "dp", split_axis=0, concat_axis=0, tiled=True)
    fetched, adapter_down_panels, adapter_up_panels = lax.optimization_barrier(
        (fetched, adapter_down_panels, adapter_up_panels)
    )
    flat_rows = fetched.reshape((owners * capacity,) + key_value_pool.shape[1:])
    row_index = jnp.clip(target * capacity + slot_index, 0, owners * capacity - 1)
    attended = attend(row_index, flat_rows, queries, fresh_key_value, live_prefix_length, blocks_per)
    base_product = jnp.dot(
        attended.reshape(req_dev * step_count, query_width),
        output_weight,
        preferred_element_type=jnp.float32,
    )
    base_product = base_product.reshape(req_dev, step_count, out_width)
    adapter = request_adapter[:, 0]
    single_panel = lax.all_gather(adapter_down_panels, "dp", axis=0, tiled=True)
    panel_count = single_panel.shape[0]
    hit_mask = (adapter[:, None] == jnp.arange(panel_count)[None, :]).astype(jnp.float32)
    every_rank = jnp.einsum(
        "qsf,nrf->qsnr", attended, single_panel, preferred_element_type=jnp.float32
    )
    rank_part = jnp.einsum("qsnr,qn->qsr", every_rank, hit_mask)
    rank_sum = lax.psum(rank_part, "mp").astype(jnp.bfloat16)
    single_panel = lax.all_gather(adapter_up_panels, "dp", axis=0, tiled=True)
    panel_count = single_panel.shape[0]
    hit_mask = (adapter[:, None] == jnp.arange(panel_count)[None, :]).astype(jnp.bfloat16)
    selected_panel = rank_sum[:, :, None, :] * hit_mask[:, None, :, None]
    adapter_sum = jnp.einsum(
        "utja,jam->utm", selected_panel, single_panel, preferred_element_type=jnp.float32
    )
    adapter_output = (adapter_sum * ADAPTER_SCALE).astype(jnp.bfloat16)
    summed_output = lax.psum_scatter(
        base_product.astype(jnp.bfloat16), "mp", scatter_dimension=2, tiled=True
    )
    return (summed_output + adapter_output.astype(jnp.float32)).astype(jnp.bfloat16)


def solution(mesh):
    in_specs = (
        P("dp", None, "mp"),
        P("dp", None, None, "mp", None),
        P("dp", None, "mp", None, None),
        P(),
        P("dp", None),
        P("dp"),
        P("dp", None),
        P("mp", None),
        P("dp", None, "mp"),
        P("dp", None, "mp"),
    )
    out_specs = P("dp", None, "mp")
    return jax.shard_map(shards, mesh=mesh, in_specs=in_specs, out_specs=out_specs, check_vma=False)
```

```python
import jax
import jax.numpy as jnp
from jax import lax
from jax.sharding import PartitionSpec as P
from jax.experimental import pallas as pl
from jax.experimental.pallas import tpu as pltpu

ADAPTER_SCALE = 2.0


def attention_kernel(idx_ref, rows_ref, q_ref, f_ref, live_ref, out_ref, *, req_blk, blocks_per, token_cap, steps, group, scale):
    i = pl.program_id(0)
    kv_groups, q_rows, _ = q_ref.shape
    cols = live_ref.shape[2]
    prefix_cols = req_blk * token_cap
    fresh_cols = req_blk * steps
    row_id = lax.broadcasted_iota(jnp.int32, (q_rows, cols), 0)
    col_id = lax.broadcasted_iota(jnp.int32, (q_rows, cols), 1)
    row_req = row_id // (steps * group)
    row_step = (row_id % (steps * group)) // group
    fresh_id = col_id - prefix_cols
    col_req = jnp.where(
        col_id < prefix_cols,
        col_id // token_cap,
        jnp.where(fresh_id < fresh_cols, fresh_id // steps, -1),
    )
    step_ok = jnp.logical_or(col_id < prefix_cols, fresh_id % steps <= row_step)
    mask = (col_req == row_req) & step_ok & (live_ref[0] > 0)
    pad_rows = cols - prefix_cols - fresh_cols
    for g in range(kv_groups):
        keys = []
        values = []
        for r in range(req_blk):
            for b in range(blocks_per):
                row = idx_ref[(i * req_blk + r) * blocks_per + b]
                keys.append(rows_ref[row, 0, g])
                values.append(rows_ref[row, 1, g])
        keys.append(f_ref[g, 0])
        values.append(f_ref[g, 1])
        if pad_rows:
            keys.append(jnp.zeros((pad_rows, keys[0].shape[1]), keys[0].dtype))
            values.append(jnp.zeros((pad_rows, values[0].shape[1]), values[0].dtype))
        key_mat = jnp.concatenate(keys, axis=0)
        value_mat = jnp.concatenate(values, axis=0)
        scores = lax.dot_general(
            q_ref[g], key_mat, (((1,), (1,)), ((), ())), preferred_element_type=jnp.float32
        ) * scale
        scores = jnp.where(mask, scores, -jnp.inf)
        top = jnp.max(scores, axis=1, keepdims=True)
        weights = jnp.exp(scores - top)
        total = jnp.sum(weights, axis=1, keepdims=True)
        probs = (weights / total).astype(jnp.bfloat16)
        out_ref[g] = jnp.dot(probs, value_mat, preferred_element_type=jnp.float32).astype(out_ref.dtype)


def attend(row_index, rows, queries, fresh_key_value, live_prefix_length, blocks_per, interpret=False):
    req_dev, steps, _ = queries.shape
    kv_groups = fresh_key_value.shape[3]
    head_dim = fresh_key_value.shape[4]
    block_len = rows.shape[3]
    group = queries.shape[2] // (kv_groups * head_dim)
    token_cap = blocks_per * block_len
    req_blk = 4
    q_rows = req_blk * steps * group
    prefix_cols = req_blk * token_cap
    fresh_cols = req_blk * steps
    cols = -(-(prefix_cols + fresh_cols) // 128) * 128
    q_t = queries.reshape(req_dev, steps, kv_groups, group, head_dim).transpose(2, 0, 1, 3, 4)
    q_t = q_t.reshape(kv_groups, req_dev * steps * group, head_dim)
    f_t = fresh_key_value.transpose(3, 2, 0, 1, 4).reshape(kv_groups, 2, req_dev * steps, head_dim)
    live = (jnp.arange(token_cap)[None, :] < live_prefix_length[:, None]).astype(jnp.int32)
    live = live.reshape(req_dev // req_blk, prefix_cols)
    extra = jnp.concatenate(
        [jnp.ones((fresh_cols,), jnp.int32), jnp.zeros((cols - prefix_cols - fresh_cols,), jnp.int32)]
    )
    live = jnp.concatenate([live, jnp.broadcast_to(extra, (req_dev // req_blk, extra.shape[0]))], axis=1)
    live = live.reshape(req_dev // req_blk, 1, cols)
    body = lambda *refs: attention_kernel(
        *refs, req_blk=req_blk, blocks_per=blocks_per, token_cap=token_cap, steps=steps,
        group=group, scale=head_dim ** (-0.5),
    )
    grid_spec = pltpu.PrefetchScalarGridSpec(
        num_scalar_prefetch=1,
        grid=(req_dev // req_blk,),
        in_specs=[
            pl.BlockSpec(rows.shape, lambda i, idx: (0, 0, 0, 0, 0)),
            pl.BlockSpec((kv_groups, q_rows, head_dim), lambda i, idx: (0, i, 0)),
            pl.BlockSpec((kv_groups, 2, fresh_cols, head_dim), lambda i, idx: (0, 0, i, 0)),
            pl.BlockSpec((1, 1, cols), lambda i, idx: (i, 0, 0)),
        ],
        out_specs=pl.BlockSpec((kv_groups, q_rows, head_dim), lambda i, idx: (0, i, 0)),
    )
    out = pl.pallas_call(
        body,
        grid_spec=grid_spec,
        out_shape=jax.ShapeDtypeStruct(q_t.shape, jnp.bfloat16),
        interpret=interpret,
    )(row_index, rows, q_t, f_t, live)
    out = out.reshape(kv_groups, req_dev, steps, group, head_dim).transpose(1, 2, 0, 3, 4)
    return out.reshape(req_dev, steps, kv_groups * group * head_dim)


def shards(
    queries,
    fresh_key_value,
    key_value_pool,
    block_position_map,
    request_blocks,
    live_prefix_length,
    request_adapter,
    output_weight,
    adapter_down_panels,
    adapter_up_panels,
):
    owners = lax.axis_size("dp")
    req_dev, step_count, query_width = queries.shape
    kv_heads = fresh_key_value.shape[3]
    head_dim = fresh_key_value.shape[4]
    pool_dev = key_value_pool.shape[0]
    block_len = key_value_pool.shape[3]
    blocks_per = request_blocks.shape[1]
    entries = req_dev * blocks_per
    out_width = output_weight.shape[1]
    owner_range = jnp.arange(owners)
    positions = jnp.take(block_position_map, request_blocks.reshape(entries))
    target = positions // pool_dev
    local_slot = positions % pool_dev
    capacity = entries // owners
    entry_ids = jnp.arange(entries)
    same_block = positions[:, None] == positions[None, :]
    earlier = entry_ids[None, :] < entry_ids[:, None]
    first = jnp.logical_not(jnp.any(same_block & earlier, axis=1))
    same_owner = target[:, None] == target[None, :]
    rank = jnp.sum((same_owner & earlier & first[None, :]).astype(jnp.int32), axis=1)
    first_of = same_block & first[None, :]
    slot_index = jnp.sum(jnp.where(first_of, rank[None, :], 0), axis=1)
    key = jnp.where(first, target * capacity + rank, -1)
    table_ids = jnp.arange(owners * capacity)
    wish_table = jnp.sum(
        jnp.where(key[:, None] == table_ids[None, :], local_slot[:, None], 0), axis=0
    ).reshape(owners, capacity)
    wanted = lax.all_to_all(wish_table, "dp", split_axis=0, concat_axis=0, tiled=True)
    served = jnp.take(key_value_pool, wanted.reshape(-1), axis=0, mode="clip").reshape(
        (owners, capacity) + key_value_pool.shape[1:]
    )
    early_down = lax.all_gather(adapter_down_panels[:1], "dp", axis=0, tiled=True)
    served, early_down = lax.optimization_barrier((served, early_down))
    fetched = lax.all_to_all(served, "dp", split_axis=0, concat_axis=0, tiled=True)
    fetched, late_down, adapter_up_panels = lax.optimization_barrier(
        (fetched, adapter_down_panels[1:], adapter_up_panels)
    )
    flat_rows = fetched.reshape((owners * capacity,) + key_value_pool.shape[1:])
    row_index = jnp.clip(target * capacity + slot_index, 0, owners * capacity - 1)
    half = req_dev // 2
    pieces = []
    summed = []
    for part in range(2):
        rows_of = slice(part * half, (part + 1) * half)
        part_attended = attend(
            row_index[part * half * blocks_per:(part + 1) * half * blocks_per],
            flat_rows,
            queries[rows_of],
            fresh_key_value[rows_of],
            live_prefix_length[rows_of],
            blocks_per,
        )
        part_product = jnp.dot(
            part_attended.reshape(half * step_count, query_width),
            output_weight,
            preferred_element_type=jnp.float32,
        ).reshape(half, step_count, out_width)
        summed.append(
            lax.psum_scatter(part_product.astype(jnp.bfloat16), "mp", scatter_dimension=2, tiled=True)
        )
        pieces.append(part_attended)
    attended = jnp.concatenate(pieces, axis=0)
    summed_output = jnp.concatenate(summed, axis=0)
    adapter = request_adapter[:, 0]
    local_adapters = adapter_down_panels.shape[0]
    rank_part = 0.0
    late_down = lax.all_gather(late_down, "dp", axis=0, tiled=True)
    for low, width, panel in ((0, 1, early_down), (1, local_adapters - 1, late_down)):
        if width == 0:
            continue
        panel_ids = jnp.arange(panel.shape[0])
        hit_mask = (
            (adapter[:, None] // local_adapters == (panel_ids // width)[None, :])
            & (adapter[:, None] % local_adapters == (low + panel_ids % width)[None, :])
        ).astype(jnp.float32)
        every_rank = jnp.einsum("qsf,nrf->qsnr", attended, panel, preferred_element_type=jnp.float32)
        rank_part = rank_part + jnp.einsum("qsnr,qn->qsr", every_rank, hit_mask)
    rank_sum = lax.psum(rank_part, "mp").astype(jnp.bfloat16)
    single_panel = lax.all_gather(adapter_up_panels, "dp", axis=0, tiled=True)
    panel_count = single_panel.shape[0]
    hit_mask = (adapter[:, None] == jnp.arange(panel_count)[None, :]).astype(jnp.bfloat16)
    selected_panel = rank_sum[:, :, None, :] * hit_mask[:, None, :, None]
    adapter_sum = jnp.einsum(
        "utja,jam->utm", selected_panel, single_panel, preferred_element_type=jnp.float32
    )
    adapter_output = (adapter_sum * ADAPTER_SCALE).astype(jnp.bfloat16)
    return (summed_output + adapter_output.astype(jnp.float32)).astype(jnp.bfloat16)


def solution(mesh):
    in_specs = (
        P("dp", None, "mp"),
        P("dp", None, None, "mp", None),
        P("dp", None, "mp", None, None),
        P(),
        P("dp", None),
        P("dp"),
        P("dp", None),
        P("mp", None),
        P("dp", None, "mp"),
        P("dp", None, "mp"),
    )
    out_specs = P("dp", None, "mp")
    return jax.shard_map(shards, mesh=mesh, in_specs=in_specs, out_specs=out_specs, check_vma=False)
```

```python
import jax
import jax.numpy as jnp
from jax import lax
from jax.sharding import PartitionSpec as P
from jax.experimental import pallas as pl
from jax.experimental.pallas import tpu as pltpu

ADAPTER_SCALE = 2.0


def attention_kernel(idx_ref, rows_ref, q_ref, f_ref, live_ref, out_ref, *, req_blk, blocks_per, token_cap, steps, group, scale):
    i = pl.program_id(0)
    kv_groups, q_rows, _ = q_ref.shape
    cols = live_ref.shape[2]
    prefix_cols = req_blk * token_cap
    fresh_cols = req_blk * steps
    row_id = lax.broadcasted_iota(jnp.int32, (q_rows, cols), 0)
    col_id = lax.broadcasted_iota(jnp.int32, (q_rows, cols), 1)
    row_req = row_id // (steps * group)
    row_step = (row_id % (steps * group)) // group
    fresh_id = col_id - prefix_cols
    col_req = jnp.where(
        col_id < prefix_cols,
        col_id // token_cap,
        jnp.where(fresh_id < fresh_cols, fresh_id // steps, -1),
    )
    step_ok = jnp.logical_or(col_id < prefix_cols, fresh_id % steps <= row_step)
    mask = (col_req == row_req) & step_ok & (live_ref[0] > 0)
    pad_rows = cols - prefix_cols - fresh_cols
    for g in range(kv_groups):
        keys = []
        values = []
        for r in range(req_blk):
            for b in range(blocks_per):
                row = idx_ref[(i * req_blk + r) * blocks_per + b]
                keys.append(rows_ref[row, 0, g])
                values.append(rows_ref[row, 1, g])
        keys.append(f_ref[g, 0])
        values.append(f_ref[g, 1])
        if pad_rows:
            keys.append(jnp.zeros((pad_rows, keys[0].shape[1]), keys[0].dtype))
            values.append(jnp.zeros((pad_rows, values[0].shape[1]), values[0].dtype))
        key_mat = jnp.concatenate(keys, axis=0)
        value_mat = jnp.concatenate(values, axis=0)
        scores = lax.dot_general(
            q_ref[g], key_mat, (((1,), (1,)), ((), ())), preferred_element_type=jnp.float32
        ) * scale
        scores = jnp.where(mask, scores, -jnp.inf)
        top = jnp.max(scores, axis=1, keepdims=True)
        weights = jnp.exp(scores - top)
        total = jnp.sum(weights, axis=1, keepdims=True)
        probs = (weights / total).astype(jnp.bfloat16)
        out_ref[g] = jnp.dot(probs, value_mat, preferred_element_type=jnp.float32).astype(out_ref.dtype)


def attend(row_index, rows, queries, fresh_key_value, live_prefix_length, blocks_per, interpret=False):
    req_dev, steps, _ = queries.shape
    kv_groups = fresh_key_value.shape[3]
    head_dim = fresh_key_value.shape[4]
    block_len = rows.shape[3]
    group = queries.shape[2] // (kv_groups * head_dim)
    token_cap = blocks_per * block_len
    req_blk = 4
    q_rows = req_blk * steps * group
    prefix_cols = req_blk * token_cap
    fresh_cols = req_blk * steps
    cols = -(-(prefix_cols + fresh_cols) // 128) * 128
    q_t = queries.reshape(req_dev, steps, kv_groups, group, head_dim).transpose(2, 0, 1, 3, 4)
    q_t = q_t.reshape(kv_groups, req_dev * steps * group, head_dim)
    f_t = fresh_key_value.transpose(3, 2, 0, 1, 4).reshape(kv_groups, 2, req_dev * steps, head_dim)
    live = (jnp.arange(token_cap)[None, :] < live_prefix_length[:, None]).astype(jnp.int32)
    live = live.reshape(req_dev // req_blk, prefix_cols)
    extra = jnp.concatenate(
        [jnp.ones((fresh_cols,), jnp.int32), jnp.zeros((cols - prefix_cols - fresh_cols,), jnp.int32)]
    )
    live = jnp.concatenate([live, jnp.broadcast_to(extra, (req_dev // req_blk, extra.shape[0]))], axis=1)
    live = live.reshape(req_dev // req_blk, 1, cols)
    body = lambda *refs: attention_kernel(
        *refs, req_blk=req_blk, blocks_per=blocks_per, token_cap=token_cap, steps=steps,
        group=group, scale=head_dim ** (-0.5),
    )
    grid_spec = pltpu.PrefetchScalarGridSpec(
        num_scalar_prefetch=1,
        grid=(req_dev // req_blk,),
        in_specs=[
            pl.BlockSpec(rows.shape, lambda i, idx: (0, 0, 0, 0, 0)),
            pl.BlockSpec((kv_groups, q_rows, head_dim), lambda i, idx: (0, i, 0)),
            pl.BlockSpec((kv_groups, 2, fresh_cols, head_dim), lambda i, idx: (0, 0, i, 0)),
            pl.BlockSpec((1, 1, cols), lambda i, idx: (i, 0, 0)),
        ],
        out_specs=pl.BlockSpec((kv_groups, q_rows, head_dim), lambda i, idx: (0, i, 0)),
    )
    out = pl.pallas_call(
        body,
        grid_spec=grid_spec,
        out_shape=jax.ShapeDtypeStruct(q_t.shape, jnp.bfloat16),
        interpret=interpret,
    )(row_index, rows, q_t, f_t, live)
    out = out.reshape(kv_groups, req_dev, steps, group, head_dim).transpose(1, 2, 0, 3, 4)
    return out.reshape(req_dev, steps, kv_groups * group * head_dim)


def shards(
    queries,
    fresh_key_value,
    key_value_pool,
    block_position_map,
    request_blocks,
    live_prefix_length,
    request_adapter,
    output_weight,
    adapter_down_panels,
    adapter_up_panels,
):
    owners = lax.axis_size("dp")
    req_dev, step_count, query_width = queries.shape
    kv_heads = fresh_key_value.shape[3]
    head_dim = fresh_key_value.shape[4]
    pool_dev = key_value_pool.shape[0]
    block_len = key_value_pool.shape[3]
    blocks_per = request_blocks.shape[1]
    entries = req_dev * blocks_per
    out_width = output_weight.shape[1]
    owner_range = jnp.arange(owners)
    positions = jnp.take(block_position_map, request_blocks.reshape(entries))
    target = positions // pool_dev
    local_slot = positions % pool_dev
    capacity = entries // owners
    entry_ids = jnp.arange(entries)
    same_block = positions[:, None] == positions[None, :]
    earlier = entry_ids[None, :] < entry_ids[:, None]
    first = jnp.logical_not(jnp.any(same_block & earlier, axis=1))
    same_owner = target[:, None] == target[None, :]
    rank = jnp.sum((same_owner & earlier & first[None, :]).astype(jnp.int32), axis=1)
    first_of = same_block & first[None, :]
    slot_index = jnp.sum(jnp.where(first_of, rank[None, :], 0), axis=1)
    key = jnp.where(first, target * capacity + rank, -1)
    table_ids = jnp.arange(owners * capacity)
    wish_table = jnp.sum(
        jnp.where(key[:, None] == table_ids[None, :], local_slot[:, None], 0), axis=0
    ).reshape(owners, capacity)
    wanted = lax.all_to_all(wish_table, "dp", split_axis=0, concat_axis=0, tiled=True)
    served = jnp.take(key_value_pool, wanted.reshape(-1), axis=0, mode="clip").reshape(
        (owners, capacity) + key_value_pool.shape[1:]
    )
    fetched = lax.all_to_all(served, "dp", split_axis=0, concat_axis=0, tiled=True)
    fetched, adapter_down_panels, adapter_up_panels = lax.optimization_barrier(
        (fetched, adapter_down_panels, adapter_up_panels)
    )
    flat_rows = fetched.reshape((owners * capacity,) + key_value_pool.shape[1:])
    row_index = jnp.clip(target * capacity + slot_index, 0, owners * capacity - 1)
    attended = attend(row_index, flat_rows, queries, fresh_key_value, live_prefix_length, blocks_per)
    base_product = jnp.dot(
        attended.reshape(req_dev * step_count, query_width),
        output_weight,
        preferred_element_type=jnp.float32,
    )
    base_product = base_product.reshape(req_dev, step_count, out_width)
    adapter = request_adapter[:, 0]
    single_panel = lax.all_gather(adapter_down_panels, "dp", axis=0, tiled=True)
    panel_count = single_panel.shape[0]
    hit_mask = (adapter[:, None] == jnp.arange(panel_count)[None, :]).astype(jnp.float32)
    every_rank = jnp.einsum(
        "qsf,nrf->qsnr", attended, single_panel, preferred_element_type=jnp.float32
    )
    rank_part = jnp.einsum("qsnr,qn->qsr", every_rank, hit_mask)
    rank_sum = lax.psum(rank_part, "mp").astype(jnp.bfloat16)
    single_panel = lax.all_gather(adapter_up_panels, "dp", axis=0, tiled=True)
    panel_count = single_panel.shape[0]
    hit_mask = (adapter[:, None] == jnp.arange(panel_count)[None, :]).astype(jnp.bfloat16)
    selected_panel = rank_sum[:, :, None, :] * hit_mask[:, None, :, None]
    adapter_sum = jnp.einsum(
        "utja,jam->utm", selected_panel, single_panel, preferred_element_type=jnp.float32
    )
    adapter_output = (adapter_sum * ADAPTER_SCALE).astype(jnp.bfloat16)
    summed_output = lax.psum_scatter(
        base_product.astype(jnp.bfloat16), "mp", scatter_dimension=2, tiled=True
    )
    return (summed_output + adapter_output.astype(jnp.float32)).astype(jnp.bfloat16)


def solution(mesh):
    in_specs = (
        P("dp", None, "mp"),
        P("dp", None, None, "mp", None),
        P("dp", None, "mp", None, None),
        P(),
        P("dp", None),
        P("dp"),
        P("dp", None),
        P("mp", None),
        P("dp", None, "mp"),
        P("dp", None, "mp"),
    )
    out_specs = P("dp", None, "mp")
    return jax.shard_map(shards, mesh=mesh, in_specs=in_specs, out_specs=out_specs, check_vma=False)
```

```python
import jax
import jax.numpy as jnp
from jax import lax
from jax.sharding import PartitionSpec as P
from jax.experimental import pallas as pl
from jax.experimental.pallas import tpu as pltpu

ADAPTER_SCALE = 2.0


def attention_kernel(idx_ref, rows_ref, q_ref, f_ref, live_ref, out_ref, *, req_blk, blocks_per, token_cap, steps, group, scale):
    i = pl.program_id(0)
    kv_groups, q_rows, _ = q_ref.shape
    cols = live_ref.shape[2]
    prefix_cols = req_blk * token_cap
    fresh_cols = req_blk * steps
    row_id = lax.broadcasted_iota(jnp.int32, (q_rows, cols), 0)
    col_id = lax.broadcasted_iota(jnp.int32, (q_rows, cols), 1)
    row_req = row_id // (steps * group)
    row_step = (row_id % (steps * group)) // group
    fresh_id = col_id - prefix_cols
    col_req = jnp.where(
        col_id < prefix_cols,
        col_id // token_cap,
        jnp.where(fresh_id < fresh_cols, fresh_id // steps, -1),
    )
    step_ok = jnp.logical_or(col_id < prefix_cols, fresh_id % steps <= row_step)
    mask = (col_req == row_req) & step_ok & (live_ref[0] > 0)
    pad_rows = cols - prefix_cols - fresh_cols
    for g in range(kv_groups):
        keys = []
        values = []
        for r in range(req_blk):
            for b in range(blocks_per):
                row = idx_ref[(i * req_blk + r) * blocks_per + b]
                keys.append(rows_ref[row, 0, g])
                values.append(rows_ref[row, 1, g])
        keys.append(f_ref[g, 0])
        values.append(f_ref[g, 1])
        if pad_rows:
            keys.append(jnp.zeros((pad_rows, keys[0].shape[1]), keys[0].dtype))
            values.append(jnp.zeros((pad_rows, values[0].shape[1]), values[0].dtype))
        key_mat = jnp.concatenate(keys, axis=0)
        value_mat = jnp.concatenate(values, axis=0)
        scores = lax.dot_general(
            q_ref[g], key_mat, (((1,), (1,)), ((), ())), preferred_element_type=jnp.float32
        ) * scale
        scores = jnp.where(mask, scores, -jnp.inf)
        top = jnp.max(scores, axis=1, keepdims=True)
        weights = jnp.exp(scores - top)
        total = jnp.sum(weights, axis=1, keepdims=True)
        probs = (weights / total).astype(jnp.bfloat16)
        out_ref[g] = jnp.dot(probs, value_mat, preferred_element_type=jnp.float32).astype(out_ref.dtype)


def attend(row_index, rows, queries, fresh_key_value, live_prefix_length, blocks_per, interpret=False):
    req_dev, steps, _ = queries.shape
    kv_groups = fresh_key_value.shape[3]
    head_dim = fresh_key_value.shape[4]
    block_len = rows.shape[3]
    group = queries.shape[2] // (kv_groups * head_dim)
    token_cap = blocks_per * block_len
    req_blk = 4
    q_rows = req_blk * steps * group
    prefix_cols = req_blk * token_cap
    fresh_cols = req_blk * steps
    cols = -(-(prefix_cols + fresh_cols) // 128) * 128
    q_t = queries.reshape(req_dev, steps, kv_groups, group, head_dim).transpose(2, 0, 1, 3, 4)
    q_t = q_t.reshape(kv_groups, req_dev * steps * group, head_dim)
    f_t = fresh_key_value.transpose(3, 2, 0, 1, 4).reshape(kv_groups, 2, req_dev * steps, head_dim)
    live = (jnp.arange(token_cap)[None, :] < live_prefix_length[:, None]).astype(jnp.int32)
    live = live.reshape(req_dev // req_blk, prefix_cols)
    extra = jnp.concatenate(
        [jnp.ones((fresh_cols,), jnp.int32), jnp.zeros((cols - prefix_cols - fresh_cols,), jnp.int32)]
    )
    live = jnp.concatenate([live, jnp.broadcast_to(extra, (req_dev // req_blk, extra.shape[0]))], axis=1)
    live = live.reshape(req_dev // req_blk, 1, cols)
    body = lambda *refs: attention_kernel(
        *refs, req_blk=req_blk, blocks_per=blocks_per, token_cap=token_cap, steps=steps,
        group=group, scale=head_dim ** (-0.5),
    )
    grid_spec = pltpu.PrefetchScalarGridSpec(
        num_scalar_prefetch=1,
        grid=(req_dev // req_blk,),
        in_specs=[
            pl.BlockSpec(rows.shape, lambda i, idx: (0, 0, 0, 0, 0)),
            pl.BlockSpec((kv_groups, q_rows, head_dim), lambda i, idx: (0, i, 0)),
            pl.BlockSpec((kv_groups, 2, fresh_cols, head_dim), lambda i, idx: (0, 0, i, 0)),
            pl.BlockSpec((1, 1, cols), lambda i, idx: (i, 0, 0)),
        ],
        out_specs=pl.BlockSpec((kv_groups, q_rows, head_dim), lambda i, idx: (0, i, 0)),
    )
    out = pl.pallas_call(
        body,
        grid_spec=grid_spec,
        out_shape=jax.ShapeDtypeStruct(q_t.shape, jnp.bfloat16),
        interpret=interpret,
    )(row_index, rows, q_t, f_t, live)
    out = out.reshape(kv_groups, req_dev, steps, group, head_dim).transpose(1, 2, 0, 3, 4)
    return out.reshape(req_dev, steps, kv_groups * group * head_dim)


def shards(
    queries,
    fresh_key_value,
    key_value_pool,
    block_position_map,
    request_blocks,
    live_prefix_length,
    request_adapter,
    output_weight,
    adapter_down_panels,
    adapter_up_panels,
):
    owners = lax.axis_size("dp")
    req_dev, step_count, query_width = queries.shape
    kv_heads = fresh_key_value.shape[3]
    head_dim = fresh_key_value.shape[4]
    pool_dev = key_value_pool.shape[0]
    block_len = key_value_pool.shape[3]
    blocks_per = request_blocks.shape[1]
    entries = req_dev * blocks_per
    out_width = output_weight.shape[1]
    owner_range = jnp.arange(owners)
    positions = jnp.take(block_position_map, request_blocks.reshape(entries))
    target = positions // pool_dev
    local_slot = positions % pool_dev
    capacity = entries // owners
    entry_ids = jnp.arange(entries)
    same_block = positions[:, None] == positions[None, :]
    earlier = entry_ids[None, :] < entry_ids[:, None]
    first = jnp.logical_not(jnp.any(same_block & earlier, axis=1))
    same_owner = target[:, None] == target[None, :]
    rank = jnp.sum((same_owner & earlier & first[None, :]).astype(jnp.int32), axis=1)
    first_of = same_block & first[None, :]
    slot_index = jnp.sum(jnp.where(first_of, rank[None, :], 0), axis=1)
    key = jnp.where(first, target * capacity + rank, -1)
    table_ids = jnp.arange(owners * capacity)
    wish_table = jnp.sum(
        jnp.where(key[:, None] == table_ids[None, :], local_slot[:, None], 0), axis=0
    ).reshape(owners, capacity)
    me = lax.axis_index("dp")
    arrived = [wish_table[me]]
    for shift in range(1, owners):
        outgoing = jnp.take(wish_table, (me + shift) % owners, axis=0)
        arrived.append(
            lax.ppermute(outgoing, "dp", [(i, (i + shift) % owners) for i in range(owners)])
        )
    by_shift = jnp.stack(arrived)
    wanted = jnp.take(by_shift, (me - jnp.arange(owners)) % owners, axis=0)
    served = jnp.take(key_value_pool, wanted.reshape(-1), axis=0, mode="clip").reshape(
        (owners, capacity) + key_value_pool.shape[1:]
    )
    fetched = lax.all_to_all(served, "dp", split_axis=0, concat_axis=0, tiled=True)
    fetched, adapter_down_panels, adapter_up_panels = lax.optimization_barrier(
        (fetched, adapter_down_panels, adapter_up_panels)
    )
    flat_rows = fetched.reshape((owners * capacity,) + key_value_pool.shape[1:])
    row_index = jnp.clip(target * capacity + slot_index, 0, owners * capacity - 1)
    attended = attend(row_index, flat_rows, queries, fresh_key_value, live_prefix_length, blocks_per)
    base_product = jnp.dot(
        attended.reshape(req_dev * step_count, query_width),
        output_weight,
        preferred_element_type=jnp.float32,
    )
    base_product = base_product.reshape(req_dev, step_count, out_width)
    adapter = request_adapter[:, 0]
    single_panel = lax.all_gather(adapter_down_panels, "dp", axis=0, tiled=True)
    panel_count = single_panel.shape[0]
    hit_mask = (adapter[:, None] == jnp.arange(panel_count)[None, :]).astype(jnp.float32)
    every_rank = jnp.einsum(
        "qsf,nrf->qsnr", attended, single_panel, preferred_element_type=jnp.float32
    )
    rank_part = jnp.einsum("qsnr,qn->qsr", every_rank, hit_mask)
    rank_sum = lax.psum(rank_part, "mp").astype(jnp.bfloat16)
    single_panel = lax.all_gather(adapter_up_panels, "dp", axis=0, tiled=True)
    panel_count = single_panel.shape[0]
    hit_mask = (adapter[:, None] == jnp.arange(panel_count)[None, :]).astype(jnp.bfloat16)
    selected_panel = rank_sum[:, :, None, :] * hit_mask[:, None, :, None]
    adapter_sum = jnp.einsum(
        "utja,jam->utm", selected_panel, single_panel, preferred_element_type=jnp.float32
    )
    adapter_output = (adapter_sum * ADAPTER_SCALE).astype(jnp.bfloat16)
    summed_output = lax.psum_scatter(
        base_product.astype(jnp.bfloat16), "mp", scatter_dimension=2, tiled=True
    )
    return (summed_output + adapter_output.astype(jnp.float32)).astype(jnp.bfloat16)


def solution(mesh):
    in_specs = (
        P("dp", None, "mp"),
        P("dp", None, None, "mp", None),
        P("dp", None, "mp", None, None),
        P(),
        P("dp", None),
        P("dp"),
        P("dp", None),
        P("mp", None),
        P("dp", None, "mp"),
        P("dp", None, "mp"),
    )
    out_specs = P("dp", None, "mp")
    return jax.shard_map(shards, mesh=mesh, in_specs=in_specs, out_specs=out_specs, check_vma=False)
```

```python
import jax
import jax.numpy as jnp
from jax import lax
from jax.sharding import PartitionSpec as P
from jax.experimental import pallas as pl
from jax.experimental.pallas import tpu as pltpu

ADAPTER_SCALE = 2.0


def attention_kernel(idx_ref, rows_ref, q_ref, f_ref, live_ref, out_ref, *, req_blk, blocks_per, token_cap, steps, group, scale):
    i = pl.program_id(0)
    kv_groups, q_rows, _ = q_ref.shape
    cols = live_ref.shape[2]
    prefix_cols = req_blk * token_cap
    fresh_cols = req_blk * steps
    row_id = lax.broadcasted_iota(jnp.int32, (q_rows, cols), 0)
    col_id = lax.broadcasted_iota(jnp.int32, (q_rows, cols), 1)
    row_req = row_id // (steps * group)
    row_step = (row_id % (steps * group)) // group
    fresh_id = col_id - prefix_cols
    col_req = jnp.where(
        col_id < prefix_cols,
        col_id // token_cap,
        jnp.where(fresh_id < fresh_cols, fresh_id // steps, -1),
    )
    step_ok = jnp.logical_or(col_id < prefix_cols, fresh_id % steps <= row_step)
    mask = (col_req == row_req) & step_ok & (live_ref[0] > 0)
    pad_rows = cols - prefix_cols - fresh_cols
    for g in range(kv_groups):
        keys = []
        values = []
        for r in range(req_blk):
            for b in range(blocks_per):
                row = idx_ref[(i * req_blk + r) * blocks_per + b]
                keys.append(rows_ref[row, 0, g])
                values.append(rows_ref[row, 1, g])
        keys.append(f_ref[g, 0])
        values.append(f_ref[g, 1])
        if pad_rows:
            keys.append(jnp.zeros((pad_rows, keys[0].shape[1]), keys[0].dtype))
            values.append(jnp.zeros((pad_rows, values[0].shape[1]), values[0].dtype))
        key_mat = jnp.concatenate(keys, axis=0)
        value_mat = jnp.concatenate(values, axis=0)
        scores = lax.dot_general(
            q_ref[g], key_mat, (((1,), (1,)), ((), ())), preferred_element_type=jnp.float32
        ) * scale
        scores = jnp.where(mask, scores, -jnp.inf)
        top = jnp.max(scores, axis=1, keepdims=True)
        weights = jnp.exp(scores - top)
        total = jnp.sum(weights, axis=1, keepdims=True)
        probs = (weights / total).astype(jnp.bfloat16)
        out_ref[g] = jnp.dot(probs, value_mat, preferred_element_type=jnp.float32).astype(out_ref.dtype)


def attend(row_index, rows, queries, fresh_key_value, live_prefix_length, blocks_per, interpret=False):
    req_dev, steps, _ = queries.shape
    kv_groups = fresh_key_value.shape[3]
    head_dim = fresh_key_value.shape[4]
    block_len = rows.shape[3]
    group = queries.shape[2] // (kv_groups * head_dim)
    token_cap = blocks_per * block_len
    req_blk = 4
    q_rows = req_blk * steps * group
    prefix_cols = req_blk * token_cap
    fresh_cols = req_blk * steps
    cols = -(-(prefix_cols + fresh_cols) // 128) * 128
    q_t = queries.reshape(req_dev, steps, kv_groups, group, head_dim).transpose(2, 0, 1, 3, 4)
    q_t = q_t.reshape(kv_groups, req_dev * steps * group, head_dim)
    f_t = fresh_key_value.transpose(3, 2, 0, 1, 4).reshape(kv_groups, 2, req_dev * steps, head_dim)
    live = (jnp.arange(token_cap)[None, :] < live_prefix_length[:, None]).astype(jnp.int32)
    live = live.reshape(req_dev // req_blk, prefix_cols)
    extra = jnp.concatenate(
        [jnp.ones((fresh_cols,), jnp.int32), jnp.zeros((cols - prefix_cols - fresh_cols,), jnp.int32)]
    )
    live = jnp.concatenate([live, jnp.broadcast_to(extra, (req_dev // req_blk, extra.shape[0]))], axis=1)
    live = live.reshape(req_dev // req_blk, 1, cols)
    body = lambda *refs: attention_kernel(
        *refs, req_blk=req_blk, blocks_per=blocks_per, token_cap=token_cap, steps=steps,
        group=group, scale=head_dim ** (-0.5),
    )
    grid_spec = pltpu.PrefetchScalarGridSpec(
        num_scalar_prefetch=1,
        grid=(req_dev // req_blk,),
        in_specs=[
            pl.BlockSpec(rows.shape, lambda i, idx: (0, 0, 0, 0, 0)),
            pl.BlockSpec((kv_groups, q_rows, head_dim), lambda i, idx: (0, i, 0)),
            pl.BlockSpec((kv_groups, 2, fresh_cols, head_dim), lambda i, idx: (0, 0, i, 0)),
            pl.BlockSpec((1, 1, cols), lambda i, idx: (i, 0, 0)),
        ],
        out_specs=pl.BlockSpec((kv_groups, q_rows, head_dim), lambda i, idx: (0, i, 0)),
    )
    out = pl.pallas_call(
        body,
        grid_spec=grid_spec,
        out_shape=jax.ShapeDtypeStruct(q_t.shape, jnp.bfloat16),
        interpret=interpret,
    )(row_index, rows, q_t, f_t, live)
    out = out.reshape(kv_groups, req_dev, steps, group, head_dim).transpose(1, 2, 0, 3, 4)
    return out.reshape(req_dev, steps, kv_groups * group * head_dim)


def shards(
    queries,
    fresh_key_value,
    key_value_pool,
    block_position_map,
    request_blocks,
    live_prefix_length,
    request_adapter,
    output_weight,
    adapter_down_panels,
    adapter_up_panels,
):
    owners = lax.axis_size("dp")
    req_dev, step_count, query_width = queries.shape
    kv_heads = fresh_key_value.shape[3]
    head_dim = fresh_key_value.shape[4]
    pool_dev = key_value_pool.shape[0]
    block_len = key_value_pool.shape[3]
    blocks_per = request_blocks.shape[1]
    entries = req_dev * blocks_per
    out_width = output_weight.shape[1]
    owner_range = jnp.arange(owners)
    positions = jnp.take(block_position_map, request_blocks.reshape(entries))
    target = positions // pool_dev
    local_slot = positions % pool_dev
    capacity = entries // owners
    entry_ids = jnp.arange(entries)
    same_block = positions[:, None] == positions[None, :]
    earlier = entry_ids[None, :] < entry_ids[:, None]
    first = jnp.logical_not(jnp.any(same_block & earlier, axis=1))
    same_owner = target[:, None] == target[None, :]
    rank = jnp.sum((same_owner & earlier & first[None, :]).astype(jnp.int32), axis=1)
    first_of = same_block & first[None, :]
    slot_index = jnp.sum(jnp.where(first_of, rank[None, :], 0), axis=1)
    key = jnp.where(first, target * capacity + rank, -1)
    table_ids = jnp.arange(owners * capacity)
    wish_table = jnp.sum(
        jnp.where(key[:, None] == table_ids[None, :], local_slot[:, None], 0), axis=0
    ).reshape(owners, capacity)
    wanted = lax.all_to_all(wish_table, "dp", split_axis=0, concat_axis=0, tiled=True)
    me = lax.axis_index("dp")
    arrived = [jnp.take(key_value_pool, wanted[me], axis=0, mode="clip")]
    for shift in range(1, owners):
        outgoing = jnp.take(key_value_pool, wanted[(me + shift) % owners], axis=0, mode="clip")
        arrived.append(
            lax.ppermute(outgoing, "dp", [(i, (i + shift) % owners) for i in range(owners)])
        )
    flat_rows = jnp.concatenate(arrived, axis=0)
    row_index = jnp.clip(((me - target) % owners) * capacity + slot_index, 0, owners * capacity - 1)
    attended = attend(row_index, flat_rows, queries, fresh_key_value, live_prefix_length, blocks_per)
    base_product = jnp.dot(
        attended.reshape(req_dev * step_count, query_width),
        output_weight,
        preferred_element_type=jnp.float32,
    )
    base_product = base_product.reshape(req_dev, step_count, out_width)
    adapter = request_adapter[:, 0]
    single_panel = lax.all_gather(adapter_down_panels, "dp", axis=0, tiled=True)
    panel_count = single_panel.shape[0]
    hit_mask = (adapter[:, None] == jnp.arange(panel_count)[None, :]).astype(jnp.float32)
    every_rank = jnp.einsum(
        "qsf,nrf->qsnr", attended, single_panel, preferred_element_type=jnp.float32
    )
    rank_part = jnp.einsum("qsnr,qn->qsr", every_rank, hit_mask)
    rank_sum = lax.psum(rank_part, "mp").astype(jnp.bfloat16)
    single_panel = lax.all_gather(adapter_up_panels, "dp", axis=0, tiled=True)
    panel_count = single_panel.shape[0]
    hit_mask = (adapter[:, None] == jnp.arange(panel_count)[None, :]).astype(jnp.bfloat16)
    selected_panel = rank_sum[:, :, None, :] * hit_mask[:, None, :, None]
    adapter_sum = jnp.einsum(
        "utja,jam->utm", selected_panel, single_panel, preferred_element_type=jnp.float32
    )
    adapter_output = (adapter_sum * ADAPTER_SCALE).astype(jnp.bfloat16)
    summed_output = lax.psum_scatter(
        base_product.astype(jnp.bfloat16), "mp", scatter_dimension=2, tiled=True
    )
    return (summed_output + adapter_output.astype(jnp.float32)).astype(jnp.bfloat16)


def solution(mesh):
    in_specs = (
        P("dp", None, "mp"),
        P("dp", None, None, "mp", None),
        P("dp", None, "mp", None, None),
        P(),
        P("dp", None),
        P("dp"),
        P("dp", None),
        P("mp", None),
        P("dp", None, "mp"),
        P("dp", None, "mp"),
    )
    out_specs = P("dp", None, "mp")
    return jax.shard_map(shards, mesh=mesh, in_specs=in_specs, out_specs=out_specs, check_vma=False)
```

```python
import jax
import jax.numpy as jnp
from jax import lax
from jax.sharding import PartitionSpec as P
from jax.experimental import pallas as pl
from jax.experimental.pallas import tpu as pltpu

ADAPTER_SCALE = 2.0


def attention_kernel(idx_ref, rows_ref, q_ref, f_ref, live_ref, out_ref, *, req_blk, blocks_per, token_cap, steps, group, scale):
    i = pl.program_id(0)
    kv_groups, q_rows, _ = q_ref.shape
    cols = live_ref.shape[2]
    prefix_cols = req_blk * token_cap
    fresh_cols = req_blk * steps
    row_id = lax.broadcasted_iota(jnp.int32, (q_rows, cols), 0)
    col_id = lax.broadcasted_iota(jnp.int32, (q_rows, cols), 1)
    row_req = row_id // (steps * group)
    row_step = (row_id % (steps * group)) // group
    fresh_id = col_id - prefix_cols
    col_req = jnp.where(
        col_id < prefix_cols,
        col_id // token_cap,
        jnp.where(fresh_id < fresh_cols, fresh_id // steps, -1),
    )
    step_ok = jnp.logical_or(col_id < prefix_cols, fresh_id % steps <= row_step)
    mask = (col_req == row_req) & step_ok & (live_ref[0] > 0)
    pad_rows = cols - prefix_cols - fresh_cols
    for g in range(kv_groups):
        keys = []
        values = []
        for r in range(req_blk):
            for b in range(blocks_per):
                row = idx_ref[(i * req_blk + r) * blocks_per + b]
                keys.append(rows_ref[row, 0, g])
                values.append(rows_ref[row, 1, g])
        keys.append(f_ref[g, 0])
        values.append(f_ref[g, 1])
        if pad_rows:
            keys.append(jnp.zeros((pad_rows, keys[0].shape[1]), keys[0].dtype))
            values.append(jnp.zeros((pad_rows, values[0].shape[1]), values[0].dtype))
        key_mat = jnp.concatenate(keys, axis=0)
        value_mat = jnp.concatenate(values, axis=0)
        scores = lax.dot_general(
            q_ref[g], key_mat, (((1,), (1,)), ((), ())), preferred_element_type=jnp.float32
        ) * scale
        scores = jnp.where(mask, scores, -jnp.inf)
        top = jnp.max(scores, axis=1, keepdims=True)
        weights = jnp.exp(scores - top)
        total = jnp.sum(weights, axis=1, keepdims=True)
        probs = (weights / total).astype(jnp.bfloat16)
        out_ref[g] = jnp.dot(probs, value_mat, preferred_element_type=jnp.float32).astype(out_ref.dtype)


def attend(row_index, rows, queries, fresh_key_value, live_prefix_length, blocks_per, interpret=False):
    req_dev, steps, _ = queries.shape
    kv_groups = fresh_key_value.shape[3]
    head_dim = fresh_key_value.shape[4]
    block_len = rows.shape[3]
    group = queries.shape[2] // (kv_groups * head_dim)
    token_cap = blocks_per * block_len
    req_blk = 4
    q_rows = req_blk * steps * group
    prefix_cols = req_blk * token_cap
    fresh_cols = req_blk * steps
    cols = -(-(prefix_cols + fresh_cols) // 128) * 128
    q_t = queries.reshape(req_dev, steps, kv_groups, group, head_dim).transpose(2, 0, 1, 3, 4)
    q_t = q_t.reshape(kv_groups, req_dev * steps * group, head_dim)
    f_t = fresh_key_value.transpose(3, 2, 0, 1, 4).reshape(kv_groups, 2, req_dev * steps, head_dim)
    live = (jnp.arange(token_cap)[None, :] < live_prefix_length[:, None]).astype(jnp.int32)
    live = live.reshape(req_dev // req_blk, prefix_cols)
    extra = jnp.concatenate(
        [jnp.ones((fresh_cols,), jnp.int32), jnp.zeros((cols - prefix_cols - fresh_cols,), jnp.int32)]
    )
    live = jnp.concatenate([live, jnp.broadcast_to(extra, (req_dev // req_blk, extra.shape[0]))], axis=1)
    live = live.reshape(req_dev // req_blk, 1, cols)
    body = lambda *refs: attention_kernel(
        *refs, req_blk=req_blk, blocks_per=blocks_per, token_cap=token_cap, steps=steps,
        group=group, scale=head_dim ** (-0.5),
    )
    grid_spec = pltpu.PrefetchScalarGridSpec(
        num_scalar_prefetch=1,
        grid=(req_dev // req_blk,),
        in_specs=[
            pl.BlockSpec(rows.shape, lambda i, idx: (0, 0, 0, 0, 0)),
            pl.BlockSpec((kv_groups, q_rows, head_dim), lambda i, idx: (0, i, 0)),
            pl.BlockSpec((kv_groups, 2, fresh_cols, head_dim), lambda i, idx: (0, 0, i, 0)),
            pl.BlockSpec((1, 1, cols), lambda i, idx: (i, 0, 0)),
        ],
        out_specs=pl.BlockSpec((kv_groups, q_rows, head_dim), lambda i, idx: (0, i, 0)),
    )
    out = pl.pallas_call(
        body,
        grid_spec=grid_spec,
        out_shape=jax.ShapeDtypeStruct(q_t.shape, jnp.bfloat16),
        interpret=interpret,
    )(row_index, rows, q_t, f_t, live)
    out = out.reshape(kv_groups, req_dev, steps, group, head_dim).transpose(1, 2, 0, 3, 4)
    return out.reshape(req_dev, steps, kv_groups * group * head_dim)


def shards(
    queries,
    fresh_key_value,
    key_value_pool,
    block_position_map,
    request_blocks,
    live_prefix_length,
    request_adapter,
    output_weight,
    adapter_down_panels,
    adapter_up_panels,
):
    owners = lax.axis_size("dp")
    req_dev, step_count, query_width = queries.shape
    kv_heads = fresh_key_value.shape[3]
    head_dim = fresh_key_value.shape[4]
    pool_dev = key_value_pool.shape[0]
    block_len = key_value_pool.shape[3]
    blocks_per = request_blocks.shape[1]
    entries = req_dev * blocks_per
    out_width = output_weight.shape[1]
    owner_range = jnp.arange(owners)
    positions = jnp.take(block_position_map, request_blocks.reshape(entries))
    target = positions // pool_dev
    local_slot = positions % pool_dev
    capacity = entries // owners
    entry_ids = jnp.arange(entries)
    same_block = positions[:, None] == positions[None, :]
    earlier = entry_ids[None, :] < entry_ids[:, None]
    first = jnp.logical_not(jnp.any(same_block & earlier, axis=1))
    same_owner = target[:, None] == target[None, :]
    rank = jnp.sum((same_owner & earlier & first[None, :]).astype(jnp.int32), axis=1)
    first_of = same_block & first[None, :]
    slot_index = jnp.sum(jnp.where(first_of, rank[None, :], 0), axis=1)
    key = jnp.where(first, target * capacity + rank, -1)
    table_ids = jnp.arange(owners * capacity)
    wish_table = jnp.sum(
        jnp.where(key[:, None] == table_ids[None, :], local_slot[:, None], 0), axis=0
    ).reshape(owners, capacity)
    wanted = lax.all_to_all(wish_table, "dp", split_axis=0, concat_axis=0, tiled=True)
    served = jnp.take(key_value_pool, wanted.reshape(-1), axis=0, mode="clip").reshape(
        (owners, capacity) + key_value_pool.shape[1:]
    )
    fetched = lax.all_to_all(served, "dp", split_axis=0, concat_axis=0, tiled=True)
    fetched, adapter_down_panels, adapter_up_panels = lax.optimization_barrier(
        (fetched, adapter_down_panels, adapter_up_panels)
    )
    flat_rows = fetched.reshape((owners * capacity,) + key_value_pool.shape[1:])
    row_index = jnp.clip(target * capacity + slot_index, 0, owners * capacity - 1)
    attended = attend(row_index, flat_rows, queries, fresh_key_value, live_prefix_length, blocks_per)
    base_product = jnp.dot(
        attended.reshape(req_dev * step_count, query_width),
        output_weight,
        preferred_element_type=jnp.float32,
    )
    base_product = base_product.reshape(req_dev, step_count, out_width)
    adapter = request_adapter[:, 0]
    single_panel = lax.all_gather(adapter_down_panels, "dp", axis=0, tiled=True)
    panel_count = single_panel.shape[0]
    hit_mask = (adapter[:, None] == jnp.arange(panel_count)[None, :]).astype(jnp.float32)
    every_rank = jnp.einsum(
        "qsf,nrf->qsnr", attended, single_panel, preferred_element_type=jnp.float32
    )
    rank_part = jnp.einsum("qsnr,qn->qsr", every_rank, hit_mask)
    rank_sum = lax.psum(rank_part, "mp").astype(jnp.bfloat16)
    local_adapters = adapter_up_panels.shape[0]
    adapter_sum = 0.0
    for low, width in ((0, 1), (1, local_adapters - 1)):
        if width == 0:
            continue
        panel = lax.all_gather(adapter_up_panels[low:low + width], "dp", axis=0, tiled=True)
        panel_ids = jnp.arange(panel.shape[0])
        hit_mask = (
            (adapter[:, None] // local_adapters == (panel_ids // width)[None, :])
            & (adapter[:, None] % local_adapters == (low + panel_ids % width)[None, :])
        ).astype(jnp.bfloat16)
        selected_panel = rank_sum[:, :, None, :] * hit_mask[:, None, :, None]
        adapter_sum = adapter_sum + jnp.einsum(
            "utja,jam->utm", selected_panel, panel, preferred_element_type=jnp.float32
        )
    adapter_output = (adapter_sum * ADAPTER_SCALE).astype(jnp.bfloat16)
    summed_output = lax.psum_scatter(
        base_product.astype(jnp.bfloat16), "mp", scatter_dimension=2, tiled=True
    )
    return (summed_output + adapter_output.astype(jnp.float32)).astype(jnp.bfloat16)


def solution(mesh):
    in_specs = (
        P("dp", None, "mp"),
        P("dp", None, None, "mp", None),
        P("dp", None, "mp", None, None),
        P(),
        P("dp", None),
        P("dp"),
        P("dp", None),
        P("mp", None),
        P("dp", None, "mp"),
        P("dp", None, "mp"),
    )
    out_specs = P("dp", None, "mp")
    return jax.shard_map(shards, mesh=mesh, in_specs=in_specs, out_specs=out_specs, check_vma=False)
```

```python
import jax
import jax.numpy as jnp
from jax import lax
from jax.sharding import PartitionSpec as P
from jax.experimental import pallas as pl
from jax.experimental.pallas import tpu as pltpu

ADAPTER_SCALE = 2.0


def attention_kernel(idx_ref, rows_ref, q_ref, f_ref, live_ref, out_ref, *, req_blk, blocks_per, token_cap, steps, group, scale):
    i = pl.program_id(0)
    kv_groups, q_rows, _ = q_ref.shape
    cols = live_ref.shape[2]
    prefix_cols = req_blk * token_cap
    fresh_cols = req_blk * steps
    row_id = lax.broadcasted_iota(jnp.int32, (q_rows, cols), 0)
    col_id = lax.broadcasted_iota(jnp.int32, (q_rows, cols), 1)
    row_req = row_id // (steps * group)
    row_step = (row_id % (steps * group)) // group
    fresh_id = col_id - prefix_cols
    col_req = jnp.where(
        col_id < prefix_cols,
        col_id // token_cap,
        jnp.where(fresh_id < fresh_cols, fresh_id // steps, -1),
    )
    step_ok = jnp.logical_or(col_id < prefix_cols, fresh_id % steps <= row_step)
    mask = (col_req == row_req) & step_ok & (live_ref[0] > 0)
    pad_rows = cols - prefix_cols - fresh_cols
    for g in range(kv_groups):
        keys = []
        values = []
        for r in range(req_blk):
            for b in range(blocks_per):
                row = idx_ref[(i * req_blk + r) * blocks_per + b]
                keys.append(rows_ref[row, 0, g])
                values.append(rows_ref[row, 1, g])
        keys.append(f_ref[g, 0])
        values.append(f_ref[g, 1])
        if pad_rows:
            keys.append(jnp.zeros((pad_rows, keys[0].shape[1]), keys[0].dtype))
            values.append(jnp.zeros((pad_rows, values[0].shape[1]), values[0].dtype))
        key_mat = jnp.concatenate(keys, axis=0)
        value_mat = jnp.concatenate(values, axis=0)
        scores = lax.dot_general(
            q_ref[g], key_mat, (((1,), (1,)), ((), ())), preferred_element_type=jnp.float32
        ) * scale
        scores = jnp.where(mask, scores, -jnp.inf)
        top = jnp.max(scores, axis=1, keepdims=True)
        weights = jnp.exp(scores - top)
        total = jnp.sum(weights, axis=1, keepdims=True)
        probs = (weights / total).astype(jnp.bfloat16)
        out_ref[g] = jnp.dot(probs, value_mat, preferred_element_type=jnp.float32).astype(out_ref.dtype)


def attend(row_index, rows, queries, fresh_key_value, live_prefix_length, blocks_per, interpret=False):
    req_dev, steps, _ = queries.shape
    kv_groups = fresh_key_value.shape[3]
    head_dim = fresh_key_value.shape[4]
    block_len = rows.shape[3]
    group = queries.shape[2] // (kv_groups * head_dim)
    token_cap = blocks_per * block_len
    req_blk = 4
    q_rows = req_blk * steps * group
    prefix_cols = req_blk * token_cap
    fresh_cols = req_blk * steps
    cols = -(-(prefix_cols + fresh_cols) // 128) * 128
    q_t = queries.reshape(req_dev, steps, kv_groups, group, head_dim).transpose(2, 0, 1, 3, 4)
    q_t = q_t.reshape(kv_groups, req_dev * steps * group, head_dim)
    f_t = fresh_key_value.transpose(3, 2, 0, 1, 4).reshape(kv_groups, 2, req_dev * steps, head_dim)
    live = (jnp.arange(token_cap)[None, :] < live_prefix_length[:, None]).astype(jnp.int32)
    live = live.reshape(req_dev // req_blk, prefix_cols)
    extra = jnp.concatenate(
        [jnp.ones((fresh_cols,), jnp.int32), jnp.zeros((cols - prefix_cols - fresh_cols,), jnp.int32)]
    )
    live = jnp.concatenate([live, jnp.broadcast_to(extra, (req_dev // req_blk, extra.shape[0]))], axis=1)
    live = live.reshape(req_dev // req_blk, 1, cols)
    body = lambda *refs: attention_kernel(
        *refs, req_blk=req_blk, blocks_per=blocks_per, token_cap=token_cap, steps=steps,
        group=group, scale=head_dim ** (-0.5),
    )
    grid_spec = pltpu.PrefetchScalarGridSpec(
        num_scalar_prefetch=1,
        grid=(req_dev // req_blk,),
        in_specs=[
            pl.BlockSpec(rows.shape, lambda i, idx: (0, 0, 0, 0, 0)),
            pl.BlockSpec((kv_groups, q_rows, head_dim), lambda i, idx: (0, i, 0)),
            pl.BlockSpec((kv_groups, 2, fresh_cols, head_dim), lambda i, idx: (0, 0, i, 0)),
            pl.BlockSpec((1, 1, cols), lambda i, idx: (i, 0, 0)),
        ],
        out_specs=pl.BlockSpec((kv_groups, q_rows, head_dim), lambda i, idx: (0, i, 0)),
    )
    out = pl.pallas_call(
        body,
        grid_spec=grid_spec,
        out_shape=jax.ShapeDtypeStruct(q_t.shape, jnp.bfloat16),
        interpret=interpret,
    )(row_index, rows, q_t, f_t, live)
    out = out.reshape(kv_groups, req_dev, steps, group, head_dim).transpose(1, 2, 0, 3, 4)
    return out.reshape(req_dev, steps, kv_groups * group * head_dim)


def shards(
    queries,
    fresh_key_value,
    key_value_pool,
    block_position_map,
    request_blocks,
    live_prefix_length,
    request_adapter,
    output_weight,
    adapter_down_panels,
    adapter_up_panels,
):
    owners = lax.axis_size("dp")
    req_dev, step_count, query_width = queries.shape
    kv_heads = fresh_key_value.shape[3]
    head_dim = fresh_key_value.shape[4]
    pool_dev = key_value_pool.shape[0]
    block_len = key_value_pool.shape[3]
    blocks_per = request_blocks.shape[1]
    entries = req_dev * blocks_per
    out_width = output_weight.shape[1]
    owner_range = jnp.arange(owners)
    positions = jnp.take(block_position_map, request_blocks.reshape(entries))
    target = positions // pool_dev
    local_slot = positions % pool_dev
    capacity = entries // owners
    entry_ids = jnp.arange(entries)
    same_block = positions[:, None] == positions[None, :]
    earlier = entry_ids[None, :] < entry_ids[:, None]
    first = jnp.logical_not(jnp.any(same_block & earlier, axis=1))
    same_owner = target[:, None] == target[None, :]
    rank = jnp.sum((same_owner & earlier & first[None, :]).astype(jnp.int32), axis=1)
    first_of = same_block & first[None, :]
    slot_index = jnp.sum(jnp.where(first_of, rank[None, :], 0), axis=1)
    key = jnp.where(first, target * capacity + rank, -1)
    table_ids = jnp.arange(owners * capacity)
    wish_table = jnp.sum(
        jnp.where(key[:, None] == table_ids[None, :], local_slot[:, None], 0), axis=0
    ).reshape(owners, capacity)
    every_wish = lax.all_gather(wish_table, "dp", axis=0)
    wanted = jnp.take(every_wish, lax.axis_index("dp"), axis=1)
    served = jnp.take(key_value_pool, wanted.reshape(-1), axis=0, mode="clip").reshape(
        (owners, capacity) + key_value_pool.shape[1:]
    )
    fetched = lax.all_to_all(served, "dp", split_axis=0, concat_axis=0, tiled=True)
    fetched, adapter_down_panels, adapter_up_panels = lax.optimization_barrier(
        (fetched, adapter_down_panels, adapter_up_panels)
    )
    flat_rows = fetched.reshape((owners * capacity,) + key_value_pool.shape[1:])
    row_index = jnp.clip(target * capacity + slot_index, 0, owners * capacity - 1)
    attended = attend(row_index, flat_rows, queries, fresh_key_value, live_prefix_length, blocks_per)
    base_product = jnp.dot(
        attended.reshape(req_dev * step_count, query_width),
        output_weight,
        preferred_element_type=jnp.float32,
    )
    base_product = base_product.reshape(req_dev, step_count, out_width)
    adapter = request_adapter[:, 0]
    single_panel = lax.all_gather(adapter_down_panels, "dp", axis=0, tiled=True)
    panel_count = single_panel.shape[0]
    hit_mask = (adapter[:, None] == jnp.arange(panel_count)[None, :]).astype(jnp.float32)
    every_rank = jnp.einsum(
        "qsf,nrf->qsnr", attended, single_panel, preferred_element_type=jnp.float32
    )
    rank_part = jnp.einsum("qsnr,qn->qsr", every_rank, hit_mask)
    rank_sum = lax.psum(rank_part, "mp").astype(jnp.bfloat16)
    single_panel = lax.all_gather(adapter_up_panels, "dp", axis=0, tiled=True)
    panel_count = single_panel.shape[0]
    hit_mask = (adapter[:, None] == jnp.arange(panel_count)[None, :]).astype(jnp.bfloat16)
    selected_panel = rank_sum[:, :, None, :] * hit_mask[:, None, :, None]
    adapter_sum = jnp.einsum(
        "utja,jam->utm", selected_panel, single_panel, preferred_element_type=jnp.float32
    )
    adapter_output = (adapter_sum * ADAPTER_SCALE).astype(jnp.bfloat16)
    summed_output = lax.psum_scatter(
        base_product.astype(jnp.bfloat16), "mp", scatter_dimension=2, tiled=True
    )
    return (summed_output + adapter_output.astype(jnp.float32)).astype(jnp.bfloat16)


def solution(mesh):
    in_specs = (
        P("dp", None, "mp"),
        P("dp", None, None, "mp", None),
        P("dp", None, "mp", None, None),
        P(),
        P("dp", None),
        P("dp"),
        P("dp", None),
        P("mp", None),
        P("dp", None, "mp"),
        P("dp", None, "mp"),
    )
    out_specs = P("dp", None, "mp")
    return jax.shard_map(shards, mesh=mesh, in_specs=in_specs, out_specs=out_specs, check_vma=False)
```
